512 devices in a mesh: seq: 256 (over z, x, y), head: 2 (over core).
Axes of the slice: x: 4, y: 8, z: 8, core: 2. Of those that a mesh axis runs over, the one named last changes fastest.
Arguments:
- query_rows: bfloat16 [131072, 8, 128], P('seq', 'head'), may hold values from -8 to 8
- key_rows: bfloat16 [131072, 8, 128], P('seq', 'head'), may hold values from -8 to 8
- value_rows: bfloat16 [131072, 8, 128], P('seq', 'head'), may hold values from -8 to 8
- out_weight: bfloat16 [8, 128, 2048], P('head'), may hold values from -0.1875 to 0.1875
Outputs:
- layer_out: bfloat16 [131072, 2048], P('seq', 'head')
The draws below stay inside these ranges and needn't reach their ends.
All inputs are finite; a program needn't handle non-finite values.
Results may differ from the reference program's by a relative error of at most 0.015.
Values may be sent and summed in bfloat16 or wider, within the bound.
No kernel may reach another device: no remote copies, remote signals or barrier semaphores. Data moves between devices by JAX's collectives and lax.ppermute only.
A program may use at most 64 MiB of HBM per device.

```python
import jax
import jax.numpy as jnp
from jax import lax

D = 2048
HEADS = 8
DH = 128
BLOCK = 128
TOK_DEV = 512
TOKENS = 131072
LEVELS = 8
N_SEQ = 256
N_HEAD = 2


def layered_rows(key, salt):
    streams = jax.random.split(jax.random.fold_in(key, salt), 7)
    values = 1.1 * jax.random.normal(streams[0], (TOKENS, HEADS, DH), jnp.float32)
    positions = jnp.arange(TOKENS, dtype=jnp.int32)
    for order, span_bits in enumerate((3, 4, 5, 6, 7, 8)):
        broad = jax.random.normal(streams[order + 1], ((TOKENS >> span_bits) + 1, HEADS, DH), jnp.float32)
        values = values + 0.775 * broad[positions >> span_bits]
    return jnp.clip(values, -8.0, 8.0)


def draw_query_rows(key, part):
    values = layered_rows(key, 11)
    return values.astype(jnp.bfloat16)


def draw_key_rows(key, part):
    values = layered_rows(key, 13)
    return values.astype(jnp.bfloat16)


def draw_value_rows(key, part):
    streams = jax.random.split(jax.random.fold_in(key, 17), 7)
    values = jax.random.normal(streams[0], (TOKENS, HEADS, DH), jnp.float32)
    positions = jnp.arange(TOKENS, dtype=jnp.int32)
    for order, span_bits in enumerate((4, 6, 8, 10, 12, 14)):
        broad = jax.random.normal(streams[order + 1], ((TOKENS >> span_bits) + 1, HEADS, DH), jnp.float32)
        values = values + 0.6 * broad[positions >> span_bits]
    return jnp.clip(values, -8.0, 8.0).astype(jnp.bfloat16)


def levels(stream_key, shape, shards, low, top_value):
    loudness = 1.0
    for dim, parts in shards:
        heights = jax.random.uniform(jax.random.fold_in(jax.random.fold_in(stream_key, 6), dim), (parts,), jnp.float32, low / len(shards), top_value / len(shards))
        loudness = loudness * jnp.repeat(jnp.exp(heights), shape[dim] // parts).reshape((-1,) + (1,) * (len(shape) - 1 - dim))
    return loudness


def gaussian(rng, extent, scale, most, pieces=(), kind=jnp.bfloat16):
    loudness = levels(rng, extent, pieces, -0.22, 0.18) if pieces else 1.0
    entries = jax.random.normal(rng, extent, jnp.float32) * scale * loudness
    return jnp.minimum(jnp.maximum(entries, -most), most).astype(kind)


def setup_inputs(seed: int = 0) -> dict:
    key_list = jax.random.split(jax.random.key(seed), 5)
    query_rows = draw_query_rows(jax.random.fold_in(key_list[4], 71), 0)
    key_rows = draw_key_rows(jax.random.fold_in(key_list[4], 71), 0)
    value_rows = draw_value_rows(jax.random.fold_in(key_list[4], 71), 0)
    out_weight = gaussian(key_list[3], (HEADS, DH, D), (HEADS * DH) ** -0.5, 0.1875, ((0, 2),))
    return {"query_rows": query_rows, "key_rows": key_rows, "value_rows": value_rows, "out_weight": out_weight}


def coarsen(source, level_index, average):
    if level_index == 0:
        return source
    count = source.shape[0] >> level_index
    grouped = source.astype(jnp.float32).reshape((count, 1 << level_index) + source.shape[1:])
    summed = jnp.sum(grouped, axis=1)
    if average:
        summed = summed / float(1 << level_index)
    return summed.astype(jnp.bfloat16)


def slot_targets(block_index, level_index):
    if level_index == 0:
        return [block_index - 1, block_index, block_index + 1]
    return [block_index - 2, block_index + 2, jnp.where(block_index % 2 == 0, block_index + 3, block_index - 3)]


def level_terms(query_head, key_head, value_head, level_index, scale):
    coarse_query = coarsen(query_head, level_index, True)
    coarse_key = coarsen(key_head, level_index, True)
    coarse_value = coarsen(value_head, level_index, False)
    total_blocks = coarse_query.shape[0] // BLOCK
    query_blocks = coarse_query.reshape(total_blocks, BLOCK, -1)
    key_blocks = coarse_key.reshape(total_blocks, BLOCK, -1)
    value_blocks = coarse_value.reshape(total_blocks, BLOCK, -1)
    block_index = jnp.arange(total_blocks, dtype=jnp.int32)
    targets = slot_targets(block_index, level_index)
    picked_keys = jnp.concatenate([key_blocks[jnp.clip(target, 0, total_blocks - 1)] for target in targets], axis=1)
    picked_values = jnp.concatenate([value_blocks[jnp.clip(target, 0, total_blocks - 1)] for target in targets], axis=1)
    valid = jnp.concatenate([jnp.repeat(((target >= 0) & (target < total_blocks))[:, None], BLOCK, axis=1) for target in targets], axis=1)
    scores = jnp.einsum("nqd,nkd->nqk", query_blocks.astype(jnp.float32), picked_keys.astype(jnp.float32)) * scale
    scores = jnp.where(valid[:, None, :], scores, -jnp.inf)
    row_peak = jnp.max(scores, axis=2, keepdims=True)
    weights = jnp.exp(scores - row_peak)
    denominator = float(1 << level_index) * jnp.sum(weights, axis=2)
    rounded = lax.optimization_barrier(weights.astype(jnp.bfloat16))
    numerator = jnp.einsum("nqk,nkd->nqd", rounded.astype(jnp.float32), picked_values.astype(jnp.float32))
    count = total_blocks * BLOCK
    return row_peak.reshape(count), numerator.reshape(count, -1), denominator.reshape(count)


def reference(query_rows, key_rows, value_rows, out_weight):
    scale = float(DH) ** -0.5

    def one_head(operands):
        query_head, key_head, value_head = operands
        expanded = []
        for level_index in range(LEVELS + 1):
            row_peak, numerator, denominator = level_terms(query_head, key_head, value_head, level_index, scale)
            factor = 1 << level_index
            expanded.append((jnp.repeat(row_peak, factor, axis=0), jnp.repeat(numerator, factor, axis=0), jnp.repeat(denominator, factor, axis=0)))
        overall = expanded[0][0]
        for entry in expanded[1:]:
            overall = jnp.maximum(overall, entry[0])
        weighted = jnp.zeros((TOKENS, DH), jnp.float32)
        total_weight = jnp.zeros((TOKENS,), jnp.float32)
        for part_peak, numerator, denominator in expanded:
            level_factor = jnp.exp(part_peak - overall)
            weighted = weighted + level_factor[:, None] * numerator
            total_weight = total_weight + level_factor * denominator
        return (weighted / total_weight[:, None]).astype(jnp.bfloat16)

    stacked = (jnp.transpose(query_rows, (1, 0, 2)), jnp.transpose(key_rows, (1, 0, 2)), jnp.transpose(value_rows, (1, 0, 2)))
    per_head = lax.map(one_head, stacked)
    attended = jnp.transpose(per_head, (1, 0, 2)).reshape(N_SEQ, TOK_DEV, N_HEAD, (HEADS // N_HEAD) * DH)
    grouped_weight = out_weight.reshape(N_HEAD, (HEADS // N_HEAD) * DH, D)

    def project(row_block):
        total = jnp.zeros((TOK_DEV, D), jnp.float32)
        for group in range(N_HEAD):
            partial_value = jnp.dot(row_block[:, group], grouped_weight[group], preferred_element_type=jnp.float32).astype(jnp.bfloat16)
            partial_value = lax.optimization_barrier(partial_value)
            total = total + partial_value.astype(jnp.float32)
        return total.astype(jnp.bfloat16)

    return lax.map(project, attended).reshape(TOKENS, D)
```

```python
import numpy as np
import jax
import jax.numpy as jnp
from jax import lax
from jax.sharding import PartitionSpec as P

BLOCK = 128
LEVEL_COUNT = 8


def shifted(value, count, steps):
    pairs = [(s, s + steps) for s in range(count) if 0 <= s + steps < count]
    return lax.ppermute(value, "seq", pairs)


def third_pairs(count, group):
    pairs = []
    for s in range(count):
        block = s // group
        target = s - 3 * group if block % 2 == 1 else s + 3 * group
        if 0 <= target < count:
            pairs.append((s, target))
    return pairs


def pooling_layout(token_count):
    row_level, row_index, offsets = [], [], {}
    offsets[1] = 0
    for r in range(token_count // 2):
        row_level.append(1)
        row_index.append(r)
    for level in range(2, LEVEL_COUNT + 1):
        offsets[level] = len(row_level)
        rows = token_count >> level
        for r in range(BLOCK):
            row_level.append(level)
            row_index.append(r if r < rows else -1)
    return np.array(row_level, np.int32), np.array(row_index, np.int32), offsets


def per_device(query_rows, key_rows, value_rows, out_weight):
    count = lax.axis_size("seq")
    device = lax.axis_index("seq")
    token_count, heads, head_size = query_rows.shape
    scale = float(head_size) ** (-0.5)
    local_blocks = token_count // BLOCK

    row_level, row_index, offsets = pooling_layout(token_count)
    tokens = lax.broadcasted_iota(jnp.int32, (row_level.shape[0], token_count), 1)
    pool = ((tokens >> row_level[:, None]) == row_index[:, None]).astype(jnp.bfloat16)
    width = heads * head_size
    stacked = jnp.concatenate(
        [
            query_rows.reshape(token_count, width),
            key_rows.reshape(token_count, width),
            value_rows.reshape(token_count, width),
        ],
        axis=1,
    )
    sums = jnp.dot(pool, stacked, preferred_element_type=jnp.float32)
    inverse = jnp.asarray((1.0 / (1 << row_level.astype(np.int64))).astype(np.float32))[:, None]
    coarse = jnp.concatenate(
        [sums[:, : 2 * width] * inverse, sums[:, 2 * width :]], axis=1
    ).astype(jnp.bfloat16)
    coarse_q = coarse[:, :width].reshape(-1, heads, head_size)
    coarse_kv = jnp.stack(
        [coarse[:, width : 2 * width], coarse[:, 2 * width :]]
    ).reshape(2, -1, heads, head_size)

    def level_kv(level):
        rows = token_count >> level
        at = offsets[level]
        return coarse_kv[:, at : at + rows]

    fine_kv = jnp.stack([key_rows, value_rows])
    first_kv = level_kv(1)
    up = jnp.concatenate([fine_kv[:, token_count - BLOCK :], first_kv], axis=1)
    down = jnp.concatenate([fine_kv[:, :BLOCK], first_kv], axis=1)
    from_left = shifted(up, count, 1)
    from_right = shifted(down, count, -1)

    pieces = {}
    for level in range(2, LEVEL_COUNT + 1):
        group = 1 << (level - 2)
        mine = level_kv(level)
        before = shifted(mine, count, 2 * group)
        after = shifted(mine, count, -2 * group)
        third = lax.ppermute(mine, "seq", third_pairs(count, group))
        pieces[level] = jnp.stack([before, after, third])

    for bit in range(LEVEL_COUNT - 2):
        members = [level for level in range(2, LEVEL_COUNT + 1) if level - 2 > bit]
        flat = jnp.concatenate([pieces[level].reshape(-1) for level in members])
        pairs = [(s, s ^ (1 << bit)) for s in range(count)]
        theirs = lax.ppermute(flat, "seq", pairs)
        at = 0
        for level in members:
            shape = pieces[level].shape
            size = pieces[level].size
            other = theirs[at : at + size].reshape(shape)
            at += size
            pieces[level] = jnp.concatenate([pieces[level], other], axis=2)

    fine_padded = jnp.concatenate(
        [from_left[:, :BLOCK], fine_kv, from_right[:, :BLOCK]], axis=1
    )
    fine_keys = jnp.stack(
        [fine_padded[:, b * BLOCK : (b + 3) * BLOCK] for b in range(local_blocks)], axis=1
    )
    left_first = from_left[:, BLOCK:]
    right_first = from_right[:, BLOCK:]
    first_even = jnp.concatenate(
        [left_first[:, :BLOCK], right_first[:, :BLOCK], right_first[:, BLOCK:]], axis=1
    )
    first_odd = jnp.concatenate(
        [left_first[:, BLOCK:], right_first[:, BLOCK:], left_first[:, :BLOCK]], axis=1
    )
    coarse_keys = jnp.stack(
        [pieces[level].transpose(1, 0, 2, 3, 4).reshape(2, 3 * BLOCK, heads, head_size)
         for level in range(2, LEVEL_COUNT + 1)],
        axis=1,
    )
    all_keys = jnp.concatenate(
        [fine_keys, first_even[:, None], first_odd[:, None], coarse_keys], axis=1
    )

    has_left = device >= 1
    has_right = device <= count - 2
    fine_index = device * local_blocks + jnp.arange(local_blocks, dtype=jnp.int32)
    fine_valid = jnp.stack(
        [fine_index >= 1, jnp.ones_like(has_left, shape=(local_blocks,)), fine_index + 1 < count * local_blocks],
        axis=1,
    )
    first_valid = jnp.stack(
        [jnp.stack([has_left, has_right, has_right]), jnp.stack([has_left, has_right, has_left])]
    )
    coarse_valid = []
    for level in range(2, LEVEL_COUNT + 1):
        group = 1 << (level - 2)
        block = device // group
        total = count // group
        even = block % 2 == 0
        coarse_valid.append(
            jnp.stack(
                [block >= 2, block + 2 < total, jnp.where(even, block + 3 < total, block >= 3)]
            )
        )
    valid = jnp.concatenate([fine_valid, first_valid, jnp.stack(coarse_valid)], axis=0)
    valid = jnp.repeat(valid, BLOCK, axis=1)

    all_queries = jnp.concatenate(
        [
            query_rows.reshape(local_blocks, BLOCK, heads, head_size),
            coarse_q.reshape(-1, BLOCK, heads, head_size),
        ],
        axis=0,
    )
    factors = jnp.asarray(
        np.array([1.0] * local_blocks + [2.0, 2.0] + [float(1 << l) for l in range(2, LEVEL_COUNT + 1)], np.float32)
    )

    scores = (
        jnp.einsum("nqhd,nkhd->nhqk", all_queries, all_keys[0], preferred_element_type=jnp.float32)
        * scale
    )
    scores = jnp.where(valid[:, None, None, :], scores, -jnp.inf)
    peak = jnp.max(scores, axis=3)
    weights = jnp.exp(scores - peak[..., None])
    denominator = factors[:, None, None] * jnp.sum(weights, axis=3)
    numerator = jnp.einsum(
        "nhqk,nkhd->nqhd", weights.astype(jnp.bfloat16), all_keys[1], preferred_element_type=jnp.float32
    )

    def expand(block_from, block_count, level):
        rows = (token_count >> level)
        m = peak[block_from : block_from + block_count].transpose(0, 2, 1).reshape(-1, heads)[:rows]
        r = denominator[block_from : block_from + block_count].transpose(0, 2, 1).reshape(-1, heads)[:rows]
        nn = numerator[block_from : block_from + block_count].reshape(-1, heads, head_size)[:rows]
        factor = 1 << level
        m = jnp.broadcast_to(m[:, None], (rows, factor, heads)).reshape(token_count, heads)
        r = jnp.broadcast_to(r[:, None], (rows, factor, heads)).reshape(token_count, heads)
        nn = jnp.broadcast_to(nn[:, None], (rows, factor, heads, head_size)).reshape(token_count, heads, head_size)
        return m, r, nn

    terms = [expand(0, local_blocks, 0), expand(local_blocks, 2, 1)]
    for level in range(2, LEVEL_COUNT + 1):
        terms.append(expand(local_blocks + level, 1, level))
    overall = terms[0][0]
    for term in terms[1:]:
        overall = jnp.maximum(overall, term[0])
    weighted = jnp.zeros((token_count, heads, head_size), jnp.float32)
    total_weight = jnp.zeros((token_count, heads), jnp.float32)
    for m, r, nn in terms:
        factor = jnp.exp(m - overall)
        weighted = weighted + factor[:, :, None] * nn
        total_weight = total_weight + factor * r
    attended = (weighted / total_weight[:, :, None]).astype(jnp.bfloat16)

    flattened = attended.reshape(token_count, heads * head_size)
    weight_flat = out_weight.reshape(heads * head_size, out_weight.shape[2])
    half = out_weight.shape[2] // 2
    core = lax.axis_index("head")
    other_weight = lax.dynamic_slice_in_dim(weight_flat, (1 - core) * half, half, axis=1)
    mine_weight = lax.dynamic_slice_in_dim(weight_flat, core * half, half, axis=1)
    other_part = jnp.dot(flattened, other_weight, preferred_element_type=jnp.float32).astype(jnp.bfloat16)
    received = lax.ppermute(other_part, "head", [(0, 1), (1, 0)])
    mine_part = jnp.dot(flattened, mine_weight, preferred_element_type=jnp.float32).astype(jnp.bfloat16)
    return (mine_part.astype(jnp.float32) + received.astype(jnp.float32)).astype(jnp.bfloat16)


def solution(mesh):
    return jax.shard_map(
        per_device,
        mesh=mesh,
        in_specs=(
            P("seq", "head", None),
            P("seq", "head", None),
            P("seq", "head", None),
            P("head", None, None),
        ),
        out_specs=P("seq", "head"),
        check_vma=False,
    )
```

```python
import numpy as np
import jax
import jax.numpy as jnp
from jax import lax
from jax.sharding import PartitionSpec as P

BLOCK = 128
LEVEL_COUNT = 8


SEQ = tuple(f"b{bit}" for bit in reversed(range(8)))


def shifted(value, count, steps):
    pairs = [(s, s + steps) for s in range(count) if 0 <= s + steps < count]
    return lax.ppermute(value, SEQ, pairs)


def third_pairs(count, group):
    pairs = []
    for s in range(count):
        block = s // group
        target = s - 3 * group if block % 2 == 1 else s + 3 * group
        if 0 <= target < count:
            pairs.append((s, target))
    return pairs


def pooling_layout(token_count):
    row_level, row_index, offsets = [], [], {}
    offsets[1] = 0
    for r in range(token_count // 2):
        row_level.append(1)
        row_index.append(r)
    for level in range(2, LEVEL_COUNT + 1):
        offsets[level] = len(row_level)
        rows = token_count >> level
        for r in range(BLOCK):
            row_level.append(level)
            row_index.append(r if r < rows else -1)
    return np.array(row_level, np.int32), np.array(row_index, np.int32), offsets


def per_device(query_rows, key_rows, value_rows, out_weight):
    count = 1 << len(SEQ)
    device = lax.axis_index(SEQ)
    token_count, heads, head_size = query_rows.shape
    scale = float(head_size) ** (-0.5)
    local_blocks = token_count // BLOCK

    row_level, row_index, offsets = pooling_layout(token_count)
    tokens = lax.broadcasted_iota(jnp.int32, (row_level.shape[0], token_count), 1)
    pool = ((tokens >> row_level[:, None]) == row_index[:, None]).astype(jnp.bfloat16)
    width = heads * head_size
    stacked = jnp.concatenate(
        [
            query_rows.reshape(token_count, width),
            key_rows.reshape(token_count, width),
            value_rows.reshape(token_count, width),
        ],
        axis=1,
    )
    sums = jnp.dot(pool, stacked, preferred_element_type=jnp.float32)
    inverse = jnp.asarray((1.0 / (1 << row_level.astype(np.int64))).astype(np.float32))[:, None]
    coarse = jnp.concatenate(
        [sums[:, : 2 * width] * inverse, sums[:, 2 * width :]], axis=1
    ).astype(jnp.bfloat16)
    coarse_q = coarse[:, :width].reshape(-1, heads, head_size)
    coarse_kv = jnp.stack(
        [coarse[:, width : 2 * width], coarse[:, 2 * width :]]
    ).reshape(2, -1, heads, head_size)

    def level_kv(level):
        rows = token_count >> level
        at = offsets[level]
        return coarse_kv[:, at : at + rows]

    fine_kv = jnp.stack([key_rows, value_rows])
    first_kv = level_kv(1)
    up = jnp.concatenate([fine_kv[:, token_count - BLOCK :], first_kv], axis=1)
    down = jnp.concatenate([fine_kv[:, :BLOCK], first_kv], axis=1)
    from_left = shifted(up, count, 1)
    from_right = shifted(down, count, -1)

    pieces = {}
    for level in range(2, LEVEL_COUNT + 1):
        group = 1 << (level - 2)
        mine = level_kv(level)
        before = shifted(mine, count, 2 * group)
        after = shifted(mine, count, -2 * group)
        third = lax.ppermute(mine, SEQ, third_pairs(count, group))
        pieces[level] = jnp.stack([before, after, third])

    for level in range(3, LEVEL_COUNT + 1):
        pieces[level] = lax.all_gather(pieces[level], SEQ[len(SEQ) - (level - 2) :], axis=2, tiled=True)

    fine_padded = jnp.concatenate(
        [from_left[:, :BLOCK], fine_kv, from_right[:, :BLOCK]], axis=1
    )
    fine_keys = jnp.stack(
        [fine_padded[:, b * BLOCK : (b + 3) * BLOCK] for b in range(local_blocks)], axis=1
    )
    left_first = from_left[:, BLOCK:]
    right_first = from_right[:, BLOCK:]
    first_even = jnp.concatenate(
        [left_first[:, :BLOCK], right_first[:, :BLOCK], right_first[:, BLOCK:]], axis=1
    )
    first_odd = jnp.concatenate(
        [left_first[:, BLOCK:], right_first[:, BLOCK:], left_first[:, :BLOCK]], axis=1
    )
    coarse_keys = jnp.stack(
        [pieces[level].transpose(1, 0, 2, 3, 4).reshape(2, 3 * BLOCK, heads, head_size)
         for level in range(2, LEVEL_COUNT + 1)],
        axis=1,
    )
    all_keys = jnp.concatenate(
        [fine_keys, first_even[:, None], first_odd[:, None], coarse_keys], axis=1
    )

    has_left = device >= 1
    has_right = device <= count - 2
    fine_index = device * local_blocks + jnp.arange(local_blocks, dtype=jnp.int32)
    fine_valid = jnp.stack(
        [fine_index >= 1, jnp.ones_like(has_left, shape=(local_blocks,)), fine_index + 1 < count * local_blocks],
        axis=1,
    )
    first_valid = jnp.stack(
        [jnp.stack([has_left, has_right, has_right]), jnp.stack([has_left, has_right, has_left])]
    )
    coarse_valid = []
    for level in range(2, LEVEL_COUNT + 1):
        group = 1 << (level - 2)
        block = device // group
        total = count // group
        even = block % 2 == 0
        coarse_valid.append(
            jnp.stack(
                [block >= 2, block + 2 < total, jnp.where(even, block + 3 < total, block >= 3)]
            )
        )
    valid = jnp.concatenate([fine_valid, first_valid, jnp.stack(coarse_valid)], axis=0)
    valid = jnp.repeat(valid, BLOCK, axis=1)

    all_queries = jnp.concatenate(
        [
            query_rows.reshape(local_blocks, BLOCK, heads, head_size),
            coarse_q.reshape(-1, BLOCK, heads, head_size),
        ],
        axis=0,
    )
    factors = jnp.asarray(
        np.array([1.0] * local_blocks + [2.0, 2.0] + [float(1 << l) for l in range(2, LEVEL_COUNT + 1)], np.float32)
    )

    def attend(queries, keys, values, valid, factors):
        scores = (
            jnp.einsum("nqhd,nkhd->nhqk", queries, keys, preferred_element_type=jnp.float32)
            * scale
        )
        scores = jnp.where(valid[:, None, None, :], scores, -jnp.inf)
        peak = jnp.max(scores, axis=3)
        weights = jnp.exp(scores - peak[..., None])
        denominator = factors[:, None, None] * jnp.sum(weights, axis=3)
        numerator = jnp.einsum(
            "nhqk,nkhd->nqhd", weights.astype(jnp.bfloat16), values, preferred_element_type=jnp.float32
        )
        return peak, denominator, numerator

    near = local_blocks + 3
    near_terms = attend(all_queries[:near], all_keys[0, :near], all_keys[1, :near], valid[:near], factors[:near])
    far_terms = attend(all_queries[near:], all_keys[0, near:], all_keys[1, near:], valid[near:], factors[near:])

    def expand(block_from, block_count, level):
        rows = (token_count >> level)
        peak, denominator, numerator = near_terms if block_from < near else far_terms
        block_from = block_from if block_from < near else block_from - near
        m = peak[block_from : block_from + block_count].transpose(0, 2, 1).reshape(-1, heads)[:rows]
        r = denominator[block_from : block_from + block_count].transpose(0, 2, 1).reshape(-1, heads)[:rows]
        nn = numerator[block_from : block_from + block_count].reshape(-1, heads, head_size)[:rows]
        factor = 1 << level
        m = jnp.broadcast_to(m[:, None], (rows, factor, heads)).reshape(token_count, heads)
        r = jnp.broadcast_to(r[:, None], (rows, factor, heads)).reshape(token_count, heads)
        nn = jnp.broadcast_to(nn[:, None], (rows, factor, heads, head_size)).reshape(token_count, heads, head_size)
        return m, r, nn

    terms = [expand(0, local_blocks, 0), expand(local_blocks, 2, 1)]
    for level in range(2, LEVEL_COUNT + 1):
        terms.append(expand(local_blocks + level, 1, level))
    overall = terms[0][0]
    for term in terms[1:]:
        overall = jnp.maximum(overall, term[0])
    weighted = jnp.zeros((token_count, heads, head_size), jnp.float32)
    total_weight = jnp.zeros((token_count, heads), jnp.float32)
    for m, r, nn in terms:
        factor = jnp.exp(m - overall)
        weighted = weighted + factor[:, :, None] * nn
        total_weight = total_weight + factor * r
    attended = (weighted / total_weight[:, :, None]).astype(jnp.bfloat16)

    flattened = attended.reshape(token_count, heads * head_size)
    weight_flat = out_weight.reshape(heads * head_size, out_weight.shape[2])
    half = out_weight.shape[2] // 2
    core = lax.axis_index("head")
    other_weight = lax.dynamic_slice_in_dim(weight_flat, (1 - core) * half, half, axis=1)
    mine_weight = lax.dynamic_slice_in_dim(weight_flat, core * half, half, axis=1)
    other_part = jnp.dot(flattened, other_weight, preferred_element_type=jnp.float32).astype(jnp.bfloat16)
    received = lax.ppermute(other_part, "head", [(0, 1), (1, 0)])
    mine_part = jnp.dot(flattened, mine_weight, preferred_element_type=jnp.float32).astype(jnp.bfloat16)
    return (mine_part.astype(jnp.float32) + received.astype(jnp.float32)).astype(jnp.bfloat16)


def solution(mesh):
    bits = mesh.shape["seq"].bit_length() - 1
    assert bits == len(SEQ)
    split = jax.sharding.Mesh(
        mesh.devices.reshape((2,) * bits + (mesh.shape["head"],)), SEQ + ("head",)
    )
    return jax.shard_map(
        per_device,
        mesh=split,
        in_specs=(
            P(SEQ, "head", None),
            P(SEQ, "head", None),
            P(SEQ, "head", None),
            P("head", None, None),
        ),
        out_specs=P(SEQ, "head"),
        check_vma=False,
    )
```

```python
import numpy as np
import jax
import jax.numpy as jnp
from jax import lax
from jax.sharding import PartitionSpec as P

BLOCK = 128
LEVEL_COUNT = 8


def shifted(value, count, steps):
    pairs = [(s, s + steps) for s in range(count) if 0 <= s + steps < count]
    return lax.ppermute(value, "seq", pairs)


def third_pairs(count, group):
    pairs = []
    for s in range(count):
        block = s // group
        target = s - 3 * group if block % 2 == 1 else s + 3 * group
        if 0 <= target < count:
            pairs.append((s, target))
    return pairs


def pooling_layout(token_count):
    row_level, row_index, offsets = [], [], {}
    offsets[1] = 0
    for r in range(token_count // 2):
        row_level.append(1)
        row_index.append(r)
    for level in range(2, LEVEL_COUNT + 1):
        offsets[level] = len(row_level)
        rows = token_count >> level
        for r in range(BLOCK):
            row_level.append(level)
            row_index.append(r if r < rows else -1)
    return np.array(row_level, np.int32), np.array(row_index, np.int32), offsets


def per_device(query_rows, key_rows, value_rows, out_weight):
    count = lax.axis_size("seq")
    device = lax.axis_index("seq")
    token_count, heads, head_size = query_rows.shape
    scale = float(head_size) ** (-0.5)
    local_blocks = token_count // BLOCK

    row_level, row_index, offsets = pooling_layout(token_count)
    tokens = lax.broadcasted_iota(jnp.int32, (row_level.shape[0], token_count), 1)
    pool = ((tokens >> row_level[:, None]) == row_index[:, None]).astype(jnp.bfloat16)
    width = heads * head_size
    stacked = jnp.concatenate(
        [
            query_rows.reshape(token_count, width),
            key_rows.reshape(token_count, width),
            value_rows.reshape(token_count, width),
        ],
        axis=1,
    )
    sums = jnp.dot(pool, stacked, preferred_element_type=jnp.float32)
    inverse = jnp.asarray((1.0 / (1 << row_level.astype(np.int64))).astype(np.float32))[:, None]
    coarse = jnp.concatenate(
        [sums[:, : 2 * width] * inverse, sums[:, 2 * width :]], axis=1
    ).astype(jnp.bfloat16)
    coarse_q = coarse[:, :width].reshape(-1, heads, head_size)
    coarse_kv = jnp.stack(
        [coarse[:, width : 2 * width], coarse[:, 2 * width :]]
    ).reshape(2, -1, heads, head_size)

    def level_kv(level):
        rows = token_count >> level
        at = offsets[level]
        return coarse_kv[:, at : at + rows]

    fine_kv = jnp.stack([key_rows, value_rows])
    first_kv = level_kv(1)
    up = jnp.concatenate([fine_kv[:, token_count - BLOCK :], first_kv], axis=1)
    down = jnp.concatenate([fine_kv[:, :BLOCK], first_kv], axis=1)
    from_left = shifted(up, count, 1)
    from_right = shifted(down, count, -1)

    shift_levels = list(range(2, LEVEL_COUNT - 1))
    current = {level: level_kv(level) for level in shift_levels}
    for bit in range(max(level - 2 for level in shift_levels)):
        members = [level for level in shift_levels if level - 2 > bit]
        flat = jnp.concatenate([current[level].reshape(-1) for level in members])
        pairs = [(s, s ^ (1 << bit)) for s in range(count)]
        theirs = lax.ppermute(flat, "seq", pairs)
        at = 0
        for level in members:
            shape = current[level].shape
            size = current[level].size
            other = theirs[at : at + size].reshape(shape)
            at += size
            current[level] = jnp.concatenate([current[level], other], axis=1)
    level_keys = {}
    for level in shift_levels:
        group = 1 << (level - 2)
        whole = current[level]
        before = shifted(whole, count, 2 * group)
        after = shifted(whole, count, -2 * group)
        even = (device // group) % 2 == 0
        outgoing = jnp.where(even, before, after)
        third = lax.ppermute(outgoing, "seq", [(s, s ^ group) for s in range(count)])
        level_keys[level] = jnp.concatenate([before, after, third], axis=1)

    top_levels = list(range(LEVEL_COUNT - 1, LEVEL_COUNT + 1))
    lines = lax.all_gather(
        jnp.concatenate([level_kv(level).reshape(-1) for level in top_levels]), "seq"
    )
    at = 0
    for level in top_levels:
        group = 1 << (level - 2)
        rows = token_count >> level
        size = 2 * rows * heads * head_size
        total = count // group
        block = device // group
        targets = [block - 2, block + 2, jnp.where(block % 2 == 0, block + 3, block - 3)]
        chosen = []
        for target in targets:
            part = lax.dynamic_slice_in_dim(lines, jnp.clip(target, 0, total - 1) * group, group, axis=0)
            part = part[:, at : at + size].reshape(group, 2, rows, heads, head_size)
            chosen.append(jnp.moveaxis(part, 1, 0).reshape(2, group * rows, heads, head_size))
        level_keys[level] = jnp.concatenate(chosen, axis=1)
        at += size

    fine_padded = jnp.concatenate(
        [from_left[:, :BLOCK], fine_kv, from_right[:, :BLOCK]], axis=1
    )
    fine_keys = jnp.stack(
        [fine_padded[:, b * BLOCK : (b + 3) * BLOCK] for b in range(local_blocks)], axis=1
    )
    left_first = from_left[:, BLOCK:]
    right_first = from_right[:, BLOCK:]
    first_even = jnp.concatenate(
        [left_first[:, :BLOCK], right_first[:, :BLOCK], right_first[:, BLOCK:]], axis=1
    )
    first_odd = jnp.concatenate(
        [left_first[:, BLOCK:], right_first[:, BLOCK:], left_first[:, :BLOCK]], axis=1
    )
    coarse_keys = jnp.stack([level_keys[level] for level in range(2, LEVEL_COUNT + 1)], axis=1)
    all_keys = jnp.concatenate(
        [fine_keys, first_even[:, None], first_odd[:, None], coarse_keys], axis=1
    )

    has_left = device >= 1
    has_right = device <= count - 2
    fine_index = device * local_blocks + jnp.arange(local_blocks, dtype=jnp.int32)
    fine_valid = jnp.stack(
        [fine_index >= 1, jnp.ones_like(has_left, shape=(local_blocks,)), fine_index + 1 < count * local_blocks],
        axis=1,
    )
    first_valid = jnp.stack(
        [jnp.stack([has_left, has_right, has_right]), jnp.stack([has_left, has_right, has_left])]
    )
    coarse_valid = []
    for level in range(2, LEVEL_COUNT + 1):
        group = 1 << (level - 2)
        block = device // group
        total = count // group
        even = block % 2 == 0
        coarse_valid.append(
            jnp.stack(
                [block >= 2, block + 2 < total, jnp.where(even, block + 3 < total, block >= 3)]
            )
        )
    valid = jnp.concatenate([fine_valid, first_valid, jnp.stack(coarse_valid)], axis=0)
    valid = jnp.repeat(valid, BLOCK, axis=1)

    all_queries = jnp.concatenate(
        [
            query_rows.reshape(local_blocks, BLOCK, heads, head_size),
            coarse_q.reshape(-1, BLOCK, heads, head_size),
        ],
        axis=0,
    )
    factors = jnp.asarray(
        np.array([1.0] * local_blocks + [2.0, 2.0] + [float(1 << l) for l in range(2, LEVEL_COUNT + 1)], np.float32)
    )

    def attend(queries, keys, values, valid, factors):
        scores = (
            jnp.einsum("nqhd,nkhd->nhqk", queries, keys, preferred_element_type=jnp.float32)
            * scale
        )
        scores = jnp.where(valid[:, None, None, :], scores, -jnp.inf)
        peak = jnp.max(scores, axis=3)
        weights = jnp.exp(scores - peak[..., None])
        denominator = factors[:, None, None] * jnp.sum(weights, axis=3)
        numerator = jnp.einsum(
            "nhqk,nkhd->nqhd", weights.astype(jnp.bfloat16), values, preferred_element_type=jnp.float32
        )
        return peak, denominator, numerator

    near = local_blocks + 3
    near_terms = attend(all_queries[:near], all_keys[0, :near], all_keys[1, :near], valid[:near], factors[:near])
    far_terms = attend(all_queries[near:], all_keys[0, near:], all_keys[1, near:], valid[near:], factors[near:])

    def expand(block_from, block_count, level):
        rows = (token_count >> level)
        peak, denominator, numerator = near_terms if block_from < near else far_terms
        block_from = block_from if block_from < near else block_from - near
        m = peak[block_from : block_from + block_count].transpose(0, 2, 1).reshape(-1, heads)[:rows]
        r = denominator[block_from : block_from + block_count].transpose(0, 2, 1).reshape(-1, heads)[:rows]
        nn = numerator[block_from : block_from + block_count].reshape(-1, heads, head_size)[:rows]
        factor = 1 << level
        m = jnp.broadcast_to(m[:, None], (rows, factor, heads)).reshape(token_count, heads)
        r = jnp.broadcast_to(r[:, None], (rows, factor, heads)).reshape(token_count, heads)
        nn = jnp.broadcast_to(nn[:, None], (rows, factor, heads, head_size)).reshape(token_count, heads, head_size)
        return m, r, nn

    terms = [expand(0, local_blocks, 0), expand(local_blocks, 2, 1)]
    for level in range(2, LEVEL_COUNT + 1):
        terms.append(expand(local_blocks + level, 1, level))
    overall = terms[0][0]
    for term in terms[1:]:
        overall = jnp.maximum(overall, term[0])
    weighted = jnp.zeros((token_count, heads, head_size), jnp.float32)
    total_weight = jnp.zeros((token_count, heads), jnp.float32)
    for m, r, nn in terms:
        factor = jnp.exp(m - overall)
        weighted = weighted + factor[:, :, None] * nn
        total_weight = total_weight + factor * r
    attended = (weighted / total_weight[:, :, None]).astype(jnp.bfloat16)

    flattened = attended.reshape(token_count, heads * head_size)
    weight_flat = out_weight.reshape(heads * head_size, out_weight.shape[2])
    half = out_weight.shape[2] // 2
    core = lax.axis_index("head")
    other_weight = lax.dynamic_slice_in_dim(weight_flat, (1 - core) * half, half, axis=1)
    mine_weight = lax.dynamic_slice_in_dim(weight_flat, core * half, half, axis=1)
    other_part = jnp.dot(flattened, other_weight, preferred_element_type=jnp.float32).astype(jnp.bfloat16)
    received = lax.ppermute(other_part, "head", [(0, 1), (1, 0)])
    mine_part = jnp.dot(flattened, mine_weight, preferred_element_type=jnp.float32).astype(jnp.bfloat16)
    return (mine_part.astype(jnp.float32) + received.astype(jnp.float32)).astype(jnp.bfloat16)


def solution(mesh):
    return jax.shard_map(
        per_device,
        mesh=mesh,
        in_specs=(
            P("seq", "head", None),
            P("seq", "head", None),
            P("seq", "head", None),
            P("head", None, None),
        ),
        out_specs=P("seq", "head"),
        check_vma=False,
    )
```

```python
import jax
import jax.numpy as jnp
from jax import lax
from jax.sharding import PartitionSpec as P

BLOCK = 128


def partner_2(value, axis, distance):
    mask = 2**distance
    pairs = [(source, source ^ mask) for source in range(lax.axis_size(axis))]
    return lax.ppermute(value, axis, pairs)


def with_halo(value, sides, width):
    for axis, dim in sides:
        size, length = (lax.axis_size(axis), value.shape[dim])
        up = [(i, (i + 1) % size) for i in range(size - 1)]
        down = [(j, i) for i, j in up]
        last = lax.slice_in_dim(value, length - width, length, axis=dim)
        initial = lax.slice_in_dim(value, 0, width, axis=dim)
        before = lax.ppermute(last, axis, up)
        after = lax.ppermute(initial, axis, down)
        value = jnp.concatenate([before, value, after], axis=dim)
    return value


def shifted(value, axis, steps):
    count = lax.axis_size(axis)
    initial, last = (max(0, -steps), min(count, count - steps))
    return lax.ppermute(value, axis, [(source, source + steps) for source in range(initial, last)])


def joined_along(parts, dim):
    parts = jnp.moveaxis(parts, 0, dim)
    shape = parts.shape
    return parts.reshape(*shape[:dim], shape[dim] * shape[dim + 1], *shape[dim + 2 :])


def gather_packed(arrays, axis, dims):
    ravelled = jnp.concatenate([a.reshape(-1) for a in arrays])
    lines, at, done = (lax.all_gather(ravelled, axis), 0, [])
    for a, dim in zip(arrays, dims):
        parts = lines[:, at : at + a.size].reshape(-1, *a.shape)
        done.append(joined_along(parts, dim))
        at += a.size
    return tuple(done)


def cut_along(value, dim, length):
    shape = value.shape
    parts = value.reshape(*shape[:dim], length, shape[dim] // length, *shape[dim + 1 :])
    return jnp.moveaxis(parts, dim, 0)


def summed_on_arrival(value, axis, dim):
    length = lax.axis_size(axis)
    parts = lax.all_to_all(cut_along(value, dim, length), axis, 0, 0, tiled=True)
    return jnp.sum(parts.astype(jnp.float32), axis=0)


def coarsen(source, level_index, average):
    count = source.shape[0] >> level_index
    grouped = source.astype(jnp.float32).reshape((count, 1 << level_index) + source.shape[1:])
    summed = jnp.sum(grouped, axis=1)
    if average:
        summed = summed / float(1 << level_index)
    return summed.astype(jnp.bfloat16)


def slot_targets(block_index, level_index):
    if level_index == 0:
        return [block_index - 1, block_index, block_index + 1]
    return [
        block_index - 2,
        block_index + 2,
        jnp.where(block_index % 2 == 0, block_index + 3, block_index - 3),
    ]


def slot_masks(block_index, block_total, level_index, width):
    targets = slot_targets(block_index, level_index)
    return jnp.concatenate(
        [
            jnp.repeat(((target >= 0) & (target < block_total))[:, None], width, axis=1)
            for target in targets
        ],
        axis=1,
    )


def level_attend(query_blocks, key_blocks, value_blocks, valid, level_index, scale):
    scores = (
        jnp.einsum("nqhd,nkhd->nhqk", query_blocks, key_blocks, preferred_element_type=jnp.float32)
        * scale
    )
    scores = jnp.where(valid[:, None, None, :], scores, -jnp.inf)
    row_peak = jnp.max(scores, axis=3, keepdims=True)
    weights = jnp.exp(scores - row_peak)
    denominator = float(1 << level_index) * jnp.sum(weights, axis=3)
    numerator = jnp.einsum(
        "nhqk,nkhd->nqhd",
        weights.astype(jnp.bfloat16),
        value_blocks,
        preferred_element_type=jnp.float32,
    )
    block_count = query_blocks.shape[0]
    row_count = query_blocks.shape[1]
    peak_rows = jnp.transpose(row_peak[..., 0], (0, 2, 1)).reshape(block_count * row_count, -1)
    denominator_rows = jnp.transpose(denominator, (0, 2, 1)).reshape(block_count * row_count, -1)
    numerator_rows = numerator.reshape(
        block_count * row_count, numerator.shape[2], numerator.shape[3]
    )
    return (peak_rows, numerator_rows, denominator_rows)


def upper_half(device_index, bit):
    return device_index // (1 << bit) % 2 == 1


def assemble_joint(pieces, level_list, device_index):
    current = {}
    for level_index in level_list:
        current[level_index] = pieces[level_index]
    deepest = max([level_index - 2 for level_index in level_list] + [0])
    for bit in range(deepest):
        members = [level_index for level_index in level_list if level_index - 2 > bit]
        widths = [current[level_index].shape[1] for level_index in members]
        joined = jnp.concatenate([current[level_index] for level_index in members], axis=1)
        partner = partner_2(joined, "seq", bit)
        upper = upper_half(device_index, bit)
        offset = 0
        for level_index, width in zip(members, widths):
            theirs = partner[:, offset : offset + width]
            offset = offset + width
            mine = current[level_index]
            current[level_index] = jnp.where(
                upper,
                jnp.concatenate([theirs, mine], axis=1),
                jnp.concatenate([mine, theirs], axis=1),
            )
    return current


def per_device(query_rows, key_rows, value_rows, out_weight):
    seq_count = lax.axis_size("seq")
    device_index = lax.axis_index("seq")
    token_count, head_local, head_size = query_rows.shape
    scale = float(head_size) ** (-0.5)
    top_level = seq_count.bit_length() - 1
    results = []
    local_blocks = token_count // BLOCK
    fine_pair = jnp.stack([key_rows, value_rows])
    first_queries = coarsen(query_rows, 1, True)
    first_pair = jnp.stack([coarsen(key_rows, 1, True), coarsen(value_rows, 1, False)])
    up = [(i, i + 1) for i in range(seq_count - 1)]
    down = [(j, i) for i, j in up]
    from_left = lax.ppermute(
        jnp.concatenate([fine_pair[:, token_count - BLOCK :], first_pair], axis=1), "seq", up
    )
    from_right = lax.ppermute(jnp.concatenate([fine_pair[:, :BLOCK], first_pair], axis=1), "seq", down)
    padded = jnp.concatenate([from_left[:, :BLOCK], fine_pair, from_right[:, :BLOCK]], axis=1)
    padded = padded.reshape(2, local_blocks + 2, BLOCK, head_local, head_size)
    near_keys = jnp.concatenate(
        [
            padded[:, 0:local_blocks],
            padded[:, 1 : local_blocks + 1],
            padded[:, 2 : local_blocks + 2],
        ],
        axis=2,
    )
    fine_index = device_index * local_blocks + jnp.arange(local_blocks, dtype=jnp.int32)
    valid = slot_masks(fine_index, local_blocks * seq_count, 0, BLOCK)
    results.append(
        (
            0,
            level_attend(
                query_rows.reshape(local_blocks, BLOCK, head_local, head_size),
                near_keys[0],
                near_keys[1],
                valid,
                0,
                scale,
            ),
        )
    )
    half_blocks = local_blocks // 2
    padded = jnp.concatenate([from_left[:, BLOCK:], first_pair, from_right[:, BLOCK:]], axis=1)
    padded = padded.reshape(2, 3 * half_blocks, BLOCK, head_local, head_size)
    third_slot = jnp.stack([padded[:, 5], padded[:, 0]], axis=1)
    far_keys = jnp.concatenate([padded[:, 0:2], padded[:, 4:6], third_slot], axis=2)
    first_index = device_index * half_blocks + jnp.arange(half_blocks, dtype=jnp.int32)
    valid = slot_masks(first_index, half_blocks * seq_count, 1, BLOCK)
    results.append(
        (
            1,
            level_attend(
                first_queries.reshape(half_blocks, BLOCK, head_local, head_size),
                far_keys[0],
                far_keys[1],
                valid,
                1,
                scale,
            ),
        )
    )
    queries_at = {}
    pieces = {}
    for level_index in range(2, top_level + 1):
        queries_at[level_index] = coarsen(query_rows, level_index, True)
        pieces[level_index] = jnp.stack(
            [coarsen(key_rows, level_index, True), coarsen(value_rows, level_index, False)]
        )
    shift_levels = list(range(2, top_level - 1))
    assembled = assemble_joint(pieces, shift_levels, device_index)
    for level_index in shift_levels:
        group = 1 << level_index - 2
        whole_block = assembled[level_index]
        before_two = shifted(whole_block, "seq", 2 * group)
        after_two = shifted(whole_block, "seq", -2 * group)
        block_index = device_index // group
        outgoing = jnp.where(block_index % 2 == 0, before_two, after_two)
        third_block = partner_2(outgoing, "seq", level_index - 2)
        level_keys = jnp.concatenate([before_two, after_two, third_block], axis=1)[:, None]
        valid = slot_masks(jnp.reshape(block_index, (1,)), seq_count // group, level_index, BLOCK)
        results.append(
            (
                level_index,
                level_attend(
                    queries_at[level_index][None],
                    level_keys[0],
                    level_keys[1],
                    valid,
                    level_index,
                    scale,
                ),
            )
        )
    coarse_list = [top_level - 1, top_level]
    lines = lax.all_gather(
        jnp.concatenate([pieces[level_index].reshape(-1) for level_index in coarse_list]), "seq"
    )
    at = 0
    for level_index in coarse_list:
        group = 1 << level_index - 2
        block_total = seq_count // group
        rows = pieces[level_index].shape[1]
        size = pieces[level_index].size
        block_index = device_index // group
        targets = slot_targets(block_index, level_index)
        chosen = []
        for target in targets:
            part = lax.dynamic_slice_in_dim(
                lines, jnp.clip(target, 0, block_total - 1) * group, group, axis=0
            )
            part = part[:, at : at + size].reshape(group, 2, rows, head_local, head_size)
            chosen.append(jnp.moveaxis(part, 1, 0).reshape(2, group * rows, head_local, head_size))
        at += size
        level_keys = jnp.concatenate(chosen, axis=1)[:, None]
        valid = slot_masks(jnp.reshape(block_index, (1,)), block_total, level_index, BLOCK)
        results.append(
            (
                level_index,
                level_attend(
                    queries_at[level_index][None],
                    level_keys[0],
                    level_keys[1],
                    valid,
                    level_index,
                    scale,
                ),
            )
        )
    expanded = []
    for level_index, terms in results:
        factor = 1 << level_index
        expanded.append(
            (
                jnp.repeat(terms[0], factor, axis=0),
                jnp.repeat(terms[1], factor, axis=0),
                jnp.repeat(terms[2], factor, axis=0),
            )
        )
    overall = expanded[0][0]
    for entry in expanded[1:]:
        overall = jnp.maximum(overall, entry[0])
    weighted = jnp.zeros((token_count, head_local, head_size), jnp.float32)
    total_weight = jnp.zeros((token_count, head_local), jnp.float32)
    for part_peak, numerator, denominator in expanded:
        level_factor = jnp.exp(part_peak - overall)
        weighted = weighted + level_factor[:, :, None] * numerator
        total_weight = total_weight + level_factor * denominator
    attended = (weighted / total_weight[:, :, None]).astype(jnp.bfloat16)
    flattened = attended.reshape(token_count, head_local * head_size)
    weight_flat = out_weight.reshape(head_local * head_size, out_weight.shape[2])
    partial_value = jnp.dot(flattened, weight_flat, preferred_element_type=jnp.float32)
    return summed_on_arrival(partial_value.astype(jnp.bfloat16), "head", 1).astype(jnp.bfloat16)


def solution(mesh):
    return jax.shard_map(
        per_device,
        mesh=mesh,
        in_specs=(
            P("seq", "head", None),
            P("seq", "head", None),
            P("seq", "head", None),
            P("head", None, None),
        ),
        out_specs=P("seq", "head"),
        check_vma=False,
    )
```

```python
import jax
import jax.numpy as jnp
from jax import lax
from jax.sharding import PartitionSpec as P

BLOCK = 128


def partner_2(value, axis, distance):
    mask = 2**distance
    pairs = [(source, source ^ mask) for source in range(lax.axis_size(axis))]
    return lax.ppermute(value, axis, pairs)


def with_halo(value, sides, width):
    for axis, dim in sides:
        size, length = (lax.axis_size(axis), value.shape[dim])
        up = [(i, (i + 1) % size) for i in range(size - 1)]
        down = [(j, i) for i, j in up]
        last = lax.slice_in_dim(value, length - width, length, axis=dim)
        initial = lax.slice_in_dim(value, 0, width, axis=dim)
        before = lax.ppermute(last, axis, up)
        after = lax.ppermute(initial, axis, down)
        value = jnp.concatenate([before, value, after], axis=dim)
    return value


def shifted(value, axis, steps):
    count = lax.axis_size(axis)
    initial, last = (max(0, -steps), min(count, count - steps))
    return lax.ppermute(value, axis, [(source, source + steps) for source in range(initial, last)])


def joined_along(parts, dim):
    parts = jnp.moveaxis(parts, 0, dim)
    shape = parts.shape
    return parts.reshape(*shape[:dim], shape[dim] * shape[dim + 1], *shape[dim + 2 :])


def gather_packed(arrays, axis, dims):
    ravelled = jnp.concatenate([a.reshape(-1) for a in arrays])
    lines, at, done = (lax.all_gather(ravelled, axis), 0, [])
    for a, dim in zip(arrays, dims):
        parts = lines[:, at : at + a.size].reshape(-1, *a.shape)
        done.append(joined_along(parts, dim))
        at += a.size
    return tuple(done)


def cut_along(value, dim, length):
    shape = value.shape
    parts = value.reshape(*shape[:dim], length, shape[dim] // length, *shape[dim + 1 :])
    return jnp.moveaxis(parts, dim, 0)


def summed_on_arrival(value, axis, dim):
    length = lax.axis_size(axis)
    parts = lax.all_to_all(cut_along(value, dim, length), axis, 0, 0, tiled=True)
    return jnp.sum(parts.astype(jnp.float32), axis=0)


def coarsen(source, level_index, average):
    count = source.shape[0] >> level_index
    grouped = source.astype(jnp.float32).reshape((count, 1 << level_index) + source.shape[1:])
    summed = jnp.sum(grouped, axis=1)
    if average:
        summed = summed / float(1 << level_index)
    return summed.astype(jnp.bfloat16)


def slot_targets(block_index, level_index):
    if level_index == 0:
        return [block_index - 1, block_index, block_index + 1]
    return [
        block_index - 2,
        block_index + 2,
        jnp.where(block_index % 2 == 0, block_index + 3, block_index - 3),
    ]


def slot_masks(block_index, block_total, level_index, width):
    targets = slot_targets(block_index, level_index)
    return jnp.concatenate(
        [
            jnp.repeat(((target >= 0) & (target < block_total))[:, None], width, axis=1)
            for target in targets
        ],
        axis=1,
    )


def level_attend(query_blocks, key_blocks, value_blocks, valid, level_index, scale):
    scores = (
        jnp.einsum("nqhd,nkhd->nhqk", query_blocks, key_blocks, preferred_element_type=jnp.float32)
        * scale
    )
    scores = jnp.where(valid[:, None, None, :], scores, -jnp.inf)
    row_peak = jnp.max(scores, axis=3, keepdims=True)
    weights = jnp.exp(scores - row_peak)
    denominator = float(1 << level_index) * jnp.sum(weights, axis=3)
    numerator = jnp.einsum(
        "nhqk,nkhd->nqhd",
        weights.astype(jnp.bfloat16),
        value_blocks,
        preferred_element_type=jnp.float32,
    )
    block_count = query_blocks.shape[0]
    row_count = query_blocks.shape[1]
    peak_rows = jnp.transpose(row_peak[..., 0], (0, 2, 1)).reshape(block_count * row_count, -1)
    denominator_rows = jnp.transpose(denominator, (0, 2, 1)).reshape(block_count * row_count, -1)
    numerator_rows = numerator.reshape(
        block_count * row_count, numerator.shape[2], numerator.shape[3]
    )
    return (peak_rows, numerator_rows, denominator_rows)


def third_pairs(count, group):
    pairs = []
    for source in range(count):
        target = source - 3 * group if (source // group) % 2 == 1 else source + 3 * group
        if 0 <= target < count:
            pairs.append((source, target))
    return pairs


def upper_half(device_index, bit):
    return device_index // (1 << bit) % 2 == 1


def assemble_joint(pieces, level_list, device_index):
    current = {}
    for level_index in level_list:
        current[level_index] = pieces[level_index]
    deepest = max([level_index - 2 for level_index in level_list] + [0])
    for bit in range(deepest):
        members = [level_index for level_index in level_list if level_index - 2 > bit]
        widths = [current[level_index].shape[1] for level_index in members]
        joined = jnp.concatenate([current[level_index] for level_index in members], axis=1)
        partner = partner_2(joined, "seq", bit)
        upper = upper_half(device_index, bit)
        offset = 0
        for level_index, width in zip(members, widths):
            theirs = partner[:, offset : offset + width]
            offset = offset + width
            mine = current[level_index]
            current[level_index] = jnp.concatenate([mine, theirs], axis=1)
    return current


def per_device(query_rows, key_rows, value_rows, out_weight):
    seq_count = lax.axis_size("seq")
    device_index = lax.axis_index("seq")
    token_count, head_local, head_size = query_rows.shape
    scale = float(head_size) ** (-0.5)
    top_level = seq_count.bit_length() - 1
    results = []
    local_blocks = token_count // BLOCK
    padded = with_halo(jnp.stack([key_rows, value_rows]), (("seq", 1),), BLOCK)
    padded = padded.reshape(2, local_blocks + 2, BLOCK, head_local, head_size)
    near_keys = jnp.concatenate(
        [
            padded[:, 0:local_blocks],
            padded[:, 1 : local_blocks + 1],
            padded[:, 2 : local_blocks + 2],
        ],
        axis=2,
    )
    fine_index = device_index * local_blocks + jnp.arange(local_blocks, dtype=jnp.int32)
    valid = slot_masks(fine_index, local_blocks * seq_count, 0, BLOCK)
    results.append(
        (
            0,
            level_attend(
                query_rows.reshape(local_blocks, BLOCK, head_local, head_size),
                near_keys[0],
                near_keys[1],
                valid,
                0,
                scale,
            ),
        )
    )
    half_blocks = local_blocks // 2
    first_queries = coarsen(query_rows, 1, True)
    first_pair = jnp.stack([coarsen(key_rows, 1, True), coarsen(value_rows, 1, False)])
    padded = with_halo(first_pair, (("seq", 1),), first_pair.shape[1])
    padded = padded.reshape(2, 3 * half_blocks, BLOCK, head_local, head_size)
    third_slot = jnp.stack([padded[:, 5], padded[:, 0]], axis=1)
    far_keys = jnp.concatenate([padded[:, 0:2], padded[:, 4:6], third_slot], axis=2)
    first_index = device_index * half_blocks + jnp.arange(half_blocks, dtype=jnp.int32)
    valid = slot_masks(first_index, half_blocks * seq_count, 1, BLOCK)
    results.append(
        (
            1,
            level_attend(
                first_queries.reshape(half_blocks, BLOCK, head_local, head_size),
                far_keys[0],
                far_keys[1],
                valid,
                1,
                scale,
            ),
        )
    )
    queries_at = {}
    pieces = {}
    for level_index in range(2, top_level + 1):
        queries_at[level_index] = coarsen(query_rows, level_index, True)
        pieces[level_index] = jnp.stack(
            [coarsen(key_rows, level_index, True), coarsen(value_rows, level_index, False)]
        )
    shift_levels = list(range(2, top_level - 1))
    assembled = assemble_joint(pieces, shift_levels, device_index)
    for level_index in shift_levels:
        group = 1 << level_index - 2
        whole_block = assembled[level_index]
        before_two = shifted(whole_block, "seq", 2 * group)
        after_two = shifted(whole_block, "seq", -2 * group)
        block_index = device_index // group
        third_block = lax.ppermute(whole_block, "seq", third_pairs(seq_count, group))
        level_keys = jnp.concatenate([before_two, after_two, third_block], axis=1)[:, None]
        valid = slot_masks(jnp.reshape(block_index, (1,)), seq_count // group, level_index, BLOCK)
        results.append(
            (
                level_index,
                level_attend(
                    queries_at[level_index][None],
                    level_keys[0],
                    level_keys[1],
                    valid,
                    level_index,
                    scale,
                ),
            )
        )
    coarse_list = [top_level - 1, top_level]
    wholes = gather_packed((pieces[top_level - 1], pieces[top_level]), "seq", (1, 1))
    for position, level_index in enumerate(coarse_list):
        group = 1 << level_index - 2
        block_total = seq_count // group
        whole_level = wholes[position].reshape(2, block_total, BLOCK, head_local, head_size)
        block_index = device_index // group
        targets = slot_targets(block_index, level_index)
        chosen = [
            lax.dynamic_index_in_dim(
                whole_level, jnp.clip(target, 0, block_total - 1), axis=1, keepdims=False
            )
            for target in targets
        ]
        level_keys = jnp.concatenate(chosen, axis=1)[:, None]
        valid = slot_masks(jnp.reshape(block_index, (1,)), block_total, level_index, BLOCK)
        results.append(
            (
                level_index,
                level_attend(
                    queries_at[level_index][None],
                    level_keys[0],
                    level_keys[1],
                    valid,
                    level_index,
                    scale,
                ),
            )
        )
    expanded = []
    for level_index, terms in results:
        factor = 1 << level_index
        expanded.append(
            (
                jnp.repeat(terms[0], factor, axis=0),
                jnp.repeat(terms[1], factor, axis=0),
                jnp.repeat(terms[2], factor, axis=0),
            )
        )
    overall = expanded[0][0]
    for entry in expanded[1:]:
        overall = jnp.maximum(overall, entry[0])
    weighted = jnp.zeros((token_count, head_local, head_size), jnp.float32)
    total_weight = jnp.zeros((token_count, head_local), jnp.float32)
    for part_peak, numerator, denominator in expanded:
        level_factor = jnp.exp(part_peak - overall)
        weighted = weighted + level_factor[:, :, None] * numerator
        total_weight = total_weight + level_factor * denominator
    attended = (weighted / total_weight[:, :, None]).astype(jnp.bfloat16)
    flattened = attended.reshape(token_count, head_local * head_size)
    weight_flat = out_weight.reshape(head_local * head_size, out_weight.shape[2])
    half = weight_flat.shape[1] // 2
    core = lax.axis_index("head")
    other_weight = lax.dynamic_slice_in_dim(weight_flat, (1 - core) * half, half, axis=1)
    mine_weight = lax.dynamic_slice_in_dim(weight_flat, core * half, half, axis=1)
    other_part = jnp.dot(flattened, other_weight, preferred_element_type=jnp.float32)
    received = lax.ppermute(other_part.astype(jnp.bfloat16), "head", [(0, 1), (1, 0)])
    mine_part = jnp.dot(flattened, mine_weight, preferred_element_type=jnp.float32)
    total = mine_part.astype(jnp.bfloat16).astype(jnp.float32) + received.astype(jnp.float32)
    return total.astype(jnp.bfloat16)


def solution(mesh):
    return jax.shard_map(
        per_device,
        mesh=mesh,
        in_specs=(
            P("seq", "head", None),
            P("seq", "head", None),
            P("seq", "head", None),
            P("head", None, None),
        ),
        out_specs=P("seq", "head"),
        check_vma=False,
    )
```

```python
import jax
import jax.numpy as jnp
from jax import lax
from jax.sharding import PartitionSpec as P

BLOCK = 128


def partner_2(value, axis, distance):
    mask = 2**distance
    pairs = [(source, source ^ mask) for source in range(lax.axis_size(axis))]
    return lax.ppermute(value, axis, pairs)


def with_halo(value, sides, width):
    for axis, dim in sides:
        size, length = (lax.axis_size(axis), value.shape[dim])
        up = [(i, (i + 1) % size) for i in range(size - 1)]
        down = [(j, i) for i, j in up]
        last = lax.slice_in_dim(value, length - width, length, axis=dim)
        initial = lax.slice_in_dim(value, 0, width, axis=dim)
        before = lax.ppermute(last, axis, up)
        after = lax.ppermute(initial, axis, down)
        value = jnp.concatenate([before, value, after], axis=dim)
    return value


def shifted(value, axis, steps):
    count = lax.axis_size(axis)
    initial, last = (max(0, -steps), min(count, count - steps))
    return lax.ppermute(value, axis, [(source, source + steps) for source in range(initial, last)])


def joined_along(parts, dim):
    parts = jnp.moveaxis(parts, 0, dim)
    shape = parts.shape
    return parts.reshape(*shape[:dim], shape[dim] * shape[dim + 1], *shape[dim + 2 :])


def gather_packed(arrays, axis, dims):
    ravelled = jnp.concatenate([a.reshape(-1) for a in arrays])
    lines, at, done = (lax.all_gather(ravelled, axis), 0, [])
    for a, dim in zip(arrays, dims):
        parts = lines[:, at : at + a.size].reshape(-1, *a.shape)
        done.append(joined_along(parts, dim))
        at += a.size
    return tuple(done)


def cut_along(value, dim, length):
    shape = value.shape
    parts = value.reshape(*shape[:dim], length, shape[dim] // length, *shape[dim + 1 :])
    return jnp.moveaxis(parts, dim, 0)


def summed_on_arrival(value, axis, dim):
    length = lax.axis_size(axis)
    parts = lax.all_to_all(cut_along(value, dim, length), axis, 0, 0, tiled=True)
    return jnp.sum(parts.astype(jnp.float32), axis=0)


def coarsen(source, level_index, average):
    count = source.shape[0] >> level_index
    grouped = source.astype(jnp.float32).reshape((count, 1 << level_index) + source.shape[1:])
    summed = jnp.sum(grouped, axis=1)
    if average:
        summed = summed / float(1 << level_index)
    return summed.astype(jnp.bfloat16)


def slot_targets(block_index, level_index):
    if level_index == 0:
        return [block_index - 1, block_index, block_index + 1]
    return [
        block_index - 2,
        block_index + 2,
        jnp.where(block_index % 2 == 0, block_index + 3, block_index - 3),
    ]


def slot_masks(block_index, block_total, level_index, width):
    targets = slot_targets(block_index, level_index)
    return jnp.concatenate(
        [
            jnp.repeat(((target >= 0) & (target < block_total))[:, None], width, axis=1)
            for target in targets
        ],
        axis=1,
    )


def level_attend(query_blocks, key_blocks, value_blocks, valid, level_index, scale):
    scores = (
        jnp.einsum("nqhd,nkhd->nhqk", query_blocks, key_blocks, preferred_element_type=jnp.float32)
        * scale
    )
    scores = jnp.where(valid[:, None, None, :], scores, -jnp.inf)
    row_peak = jnp.max(scores, axis=3, keepdims=True)
    weights = jnp.exp(scores - row_peak)
    denominator = float(1 << level_index) * jnp.sum(weights, axis=3)
    numerator = jnp.einsum(
        "nhqk,nkhd->nqhd",
        weights.astype(jnp.bfloat16),
        value_blocks,
        preferred_element_type=jnp.float32,
    )
    block_count = query_blocks.shape[0]
    row_count = query_blocks.shape[1]
    peak_rows = jnp.transpose(row_peak[..., 0], (0, 2, 1)).reshape(block_count * row_count, -1)
    denominator_rows = jnp.transpose(denominator, (0, 2, 1)).reshape(block_count * row_count, -1)
    numerator_rows = numerator.reshape(
        block_count * row_count, numerator.shape[2], numerator.shape[3]
    )
    return (peak_rows, numerator_rows, denominator_rows)


def upper_half(device_index, bit):
    return device_index // (1 << bit) % 2 == 1


def assemble_joint(pieces, level_list, device_index):
    current = {}
    for level_index in level_list:
        current[level_index] = pieces[level_index]
    deepest = max([level_index - 2 for level_index in level_list] + [0])
    for bit in range(deepest):
        members = [level_index for level_index in level_list if level_index - 2 > bit]
        widths = [current[level_index].shape[1] for level_index in members]
        joined = jnp.concatenate([current[level_index] for level_index in members], axis=1)
        partner = partner_2(joined, "seq", bit)
        upper = upper_half(device_index, bit)
        offset = 0
        for level_index, width in zip(members, widths):
            theirs = partner[:, offset : offset + width]
            offset = offset + width
            mine = current[level_index]
            current[level_index] = jnp.concatenate([mine, theirs], axis=1)
    return current


def per_device(query_rows, key_rows, value_rows, out_weight):
    seq_count = lax.axis_size("seq")
    device_index = lax.axis_index("seq")
    token_count, head_local, head_size = query_rows.shape
    scale = float(head_size) ** (-0.5)
    top_level = seq_count.bit_length() - 1
    results = []
    local_blocks = token_count // BLOCK
    padded = with_halo(jnp.stack([key_rows, value_rows]), (("seq", 1),), BLOCK)
    padded = padded.reshape(2, local_blocks + 2, BLOCK, head_local, head_size)
    near_keys = jnp.concatenate(
        [
            padded[:, 0:local_blocks],
            padded[:, 1 : local_blocks + 1],
            padded[:, 2 : local_blocks + 2],
        ],
        axis=2,
    )
    fine_index = device_index * local_blocks + jnp.arange(local_blocks, dtype=jnp.int32)
    valid = slot_masks(fine_index, local_blocks * seq_count, 0, BLOCK)
    results.append(
        (
            0,
            level_attend(
                query_rows.reshape(local_blocks, BLOCK, head_local, head_size),
                near_keys[0],
                near_keys[1],
                valid,
                0,
                scale,
            ),
        )
    )
    half_blocks = local_blocks // 2
    first_queries = coarsen(query_rows, 1, True)
    first_pair = jnp.stack([coarsen(key_rows, 1, True), coarsen(value_rows, 1, False)])
    padded = with_halo(first_pair, (("seq", 1),), first_pair.shape[1])
    padded = padded.reshape(2, 3 * half_blocks, BLOCK, head_local, head_size)
    third_slot = jnp.stack([padded[:, 5], padded[:, 0]], axis=1)
    far_keys = jnp.concatenate([padded[:, 0:2], padded[:, 4:6], third_slot], axis=2)
    first_index = device_index * half_blocks + jnp.arange(half_blocks, dtype=jnp.int32)
    valid = slot_masks(first_index, half_blocks * seq_count, 1, BLOCK)
    results.append(
        (
            1,
            level_attend(
                first_queries.reshape(half_blocks, BLOCK, head_local, head_size),
                far_keys[0],
                far_keys[1],
                valid,
                1,
                scale,
            ),
        )
    )
    queries_at = {}
    pieces = {}
    for level_index in range(2, top_level + 1):
        queries_at[level_index] = coarsen(query_rows, level_index, True)
        pieces[level_index] = jnp.stack(
            [coarsen(key_rows, level_index, True), coarsen(value_rows, level_index, False)]
        )
    shift_levels = list(range(2, top_level - 2))
    assembled = assemble_joint(pieces, shift_levels, device_index)
    for level_index in shift_levels:
        group = 1 << level_index - 2
        whole_block = assembled[level_index]
        before_two = shifted(whole_block, "seq", 2 * group)
        after_two = shifted(whole_block, "seq", -2 * group)
        block_index = device_index // group
        outgoing = jnp.where(block_index % 2 == 0, before_two, after_two)
        third_block = partner_2(outgoing, "seq", level_index - 2)
        level_keys = jnp.concatenate([before_two, after_two, third_block], axis=1)[:, None]
        valid = slot_masks(jnp.reshape(block_index, (1,)), seq_count // group, level_index, BLOCK)
        results.append(
            (
                level_index,
                level_attend(
                    queries_at[level_index][None],
                    level_keys[0],
                    level_keys[1],
                    valid,
                    level_index,
                    scale,
                ),
            )
        )
    coarse_list = [top_level - 2, top_level - 1, top_level]
    wholes = gather_packed(tuple(pieces[level_index] for level_index in coarse_list), "seq", (1,) * len(coarse_list))
    for position, level_index in enumerate(coarse_list):
        group = 1 << level_index - 2
        block_total = seq_count // group
        whole_level = wholes[position].reshape(2, block_total, BLOCK, head_local, head_size)
        block_index = device_index // group
        targets = slot_targets(block_index, level_index)
        chosen = [
            lax.dynamic_index_in_dim(
                whole_level, jnp.clip(target, 0, block_total - 1), axis=1, keepdims=False
            )
            for target in targets
        ]
        level_keys = jnp.concatenate(chosen, axis=1)[:, None]
        valid = slot_masks(jnp.reshape(block_index, (1,)), block_total, level_index, BLOCK)
        results.append(
            (
                level_index,
                level_attend(
                    queries_at[level_index][None],
                    level_keys[0],
                    level_keys[1],
                    valid,
                    level_index,
                    scale,
                ),
            )
        )
    expanded = []
    for level_index, terms in results:
        factor = 1 << level_index
        expanded.append(
            (
                jnp.repeat(terms[0], factor, axis=0),
                jnp.repeat(terms[1], factor, axis=0),
                jnp.repeat(terms[2], factor, axis=0),
            )
        )
    overall = expanded[0][0]
    for entry in expanded[1:]:
        overall = jnp.maximum(overall, entry[0])
    weighted = jnp.zeros((token_count, head_local, head_size), jnp.float32)
    total_weight = jnp.zeros((token_count, head_local), jnp.float32)
    for part_peak, numerator, denominator in expanded:
        level_factor = jnp.exp(part_peak - overall)
        weighted = weighted + level_factor[:, :, None] * numerator
        total_weight = total_weight + level_factor * denominator
    attended = (weighted / total_weight[:, :, None]).astype(jnp.bfloat16)
    flattened = attended.reshape(token_count, head_local * head_size)
    weight_flat = out_weight.reshape(head_local * head_size, out_weight.shape[2])
    partial_value = jnp.dot(flattened, weight_flat, preferred_element_type=jnp.float32)
    return summed_on_arrival(partial_value.astype(jnp.bfloat16), "head", 1).astype(jnp.bfloat16)


def solution(mesh):
    return jax.shard_map(
        per_device,
        mesh=mesh,
        in_specs=(
            P("seq", "head", None),
            P("seq", "head", None),
            P("seq", "head", None),
            P("head", None, None),
        ),
        out_specs=P("seq", "head"),
        check_vma=False,
    )
```

```python
import jax
import jax.numpy as jnp
from jax import lax
from jax.sharding import PartitionSpec as P

BLOCK = 128


def partner_2(value, axis, distance):
    mask = 2**distance
    pairs = [(source, source ^ mask) for source in range(lax.axis_size(axis))]
    return lax.ppermute(value, axis, pairs)


def with_halo(value, sides, width):
    for axis, dim in sides:
        size, length = (lax.axis_size(axis), value.shape[dim])
        up = [(i, (i + 1) % size) for i in range(size - 1)]
        down = [(j, i) for i, j in up]
        last = lax.slice_in_dim(value, length - width, length, axis=dim)
        initial = lax.slice_in_dim(value, 0, width, axis=dim)
        before = lax.ppermute(last, axis, up)
        after = lax.ppermute(initial, axis, down)
        value = jnp.concatenate([before, value, after], axis=dim)
    return value


def shifted(value, axis, steps):
    count = lax.axis_size(axis)
    initial, last = (max(0, -steps), min(count, count - steps))
    return lax.ppermute(value, axis, [(source, source + steps) for source in range(initial, last)])


def joined_along(parts, dim):
    parts = jnp.moveaxis(parts, 0, dim)
    shape = parts.shape
    return parts.reshape(*shape[:dim], shape[dim] * shape[dim + 1], *shape[dim + 2 :])


def gather_packed(arrays, axis, dims):
    ravelled = jnp.concatenate([a.reshape(-1) for a in arrays])
    lines, at, done = (lax.all_gather(ravelled, axis), 0, [])
    for a, dim in zip(arrays, dims):
        parts = lines[:, at : at + a.size].reshape(-1, *a.shape)
        done.append(joined_along(parts, dim))
        at += a.size
    return tuple(done)


def cut_along(value, dim, length):
    shape = value.shape
    parts = value.reshape(*shape[:dim], length, shape[dim] // length, *shape[dim + 1 :])
    return jnp.moveaxis(parts, dim, 0)


def summed_on_arrival(value, axis, dim):
    length = lax.axis_size(axis)
    parts = lax.all_to_all(cut_along(value, dim, length), axis, 0, 0, tiled=True)
    return jnp.sum(parts.astype(jnp.float32), axis=0)


def coarsen(source, level_index, average):
    count = source.shape[0] >> level_index
    grouped = source.astype(jnp.float32).reshape((count, 1 << level_index) + source.shape[1:])
    summed = jnp.sum(grouped, axis=1)
    if average:
        summed = summed / float(1 << level_index)
    return summed.astype(jnp.bfloat16)


def slot_targets(block_index, level_index):
    if level_index == 0:
        return [block_index - 1, block_index, block_index + 1]
    return [
        block_index - 2,
        block_index + 2,
        jnp.where(block_index % 2 == 0, block_index + 3, block_index - 3),
    ]


def slot_masks(block_index, block_total, level_index, width):
    targets = slot_targets(block_index, level_index)
    return jnp.concatenate(
        [
            jnp.repeat(((target >= 0) & (target < block_total))[:, None], width, axis=1)
            for target in targets
        ],
        axis=1,
    )


def level_attend(query_blocks, key_blocks, value_blocks, valid, level_index, scale):
    scores = (
        jnp.einsum("nqhd,nkhd->nhqk", query_blocks, key_blocks, preferred_element_type=jnp.float32)
        * scale
    )
    scores = jnp.where(valid[:, None, None, :], scores, -jnp.inf)
    row_peak = jnp.max(scores, axis=3, keepdims=True)
    weights = jnp.exp(scores - row_peak)
    denominator = float(1 << level_index) * jnp.sum(weights, axis=3)
    numerator = jnp.einsum(
        "nhqk,nkhd->nqhd",
        weights.astype(jnp.bfloat16),
        value_blocks,
        preferred_element_type=jnp.float32,
    )
    block_count = query_blocks.shape[0]
    row_count = query_blocks.shape[1]
    peak_rows = jnp.transpose(row_peak[..., 0], (0, 2, 1)).reshape(block_count * row_count, -1)
    denominator_rows = jnp.transpose(denominator, (0, 2, 1)).reshape(block_count * row_count, -1)
    numerator_rows = numerator.reshape(
        block_count * row_count, numerator.shape[2], numerator.shape[3]
    )
    return (peak_rows, numerator_rows, denominator_rows)


def upper_half(device_index, bit):
    return device_index // (1 << bit) % 2 == 1


def assemble_joint(pieces, level_list, device_index):
    current = {}
    for level_index in level_list:
        current[level_index] = pieces[level_index]
    deepest = max([level_index - 2 for level_index in level_list] + [0])
    for bit in range(deepest):
        members = [level_index for level_index in level_list if level_index - 2 > bit]
        widths = [current[level_index].shape[1] for level_index in members]
        joined = jnp.concatenate([current[level_index] for level_index in members], axis=1)
        partner = partner_2(joined, "seq", bit)
        upper = upper_half(device_index, bit)
        offset = 0
        for level_index, width in zip(members, widths):
            theirs = partner[:, offset : offset + width]
            offset = offset + width
            mine = current[level_index]
            current[level_index] = jnp.concatenate([mine, theirs], axis=1)
    return current


def per_device(query_rows, key_rows, value_rows, out_weight):
    seq_count = lax.axis_size("seq")
    device_index = lax.axis_index("seq")
    token_count, head_local, head_size = query_rows.shape
    scale = float(head_size) ** (-0.5)
    top_level = seq_count.bit_length() - 1
    results = []
    local_blocks = token_count // BLOCK
    padded = with_halo(jnp.stack([key_rows, value_rows]), (("seq", 1),), BLOCK)
    padded = padded.reshape(2, local_blocks + 2, BLOCK, head_local, head_size)
    near_keys = jnp.concatenate(
        [
            padded[:, 0:local_blocks],
            padded[:, 1 : local_blocks + 1],
            padded[:, 2 : local_blocks + 2],
        ],
        axis=2,
    )
    fine_index = device_index * local_blocks + jnp.arange(local_blocks, dtype=jnp.int32)
    valid = slot_masks(fine_index, local_blocks * seq_count, 0, BLOCK)
    results.append(
        (
            0,
            level_attend(
                query_rows.reshape(local_blocks, BLOCK, head_local, head_size),
                near_keys[0],
                near_keys[1],
                valid,
                0,
                scale,
            ),
        )
    )
    half_blocks = local_blocks // 2
    first_queries = coarsen(query_rows, 1, True)
    first_pair = jnp.stack([coarsen(key_rows, 1, True), coarsen(value_rows, 1, False)])
    padded = with_halo(first_pair, (("seq", 1),), first_pair.shape[1])
    padded = padded.reshape(2, 3 * half_blocks, BLOCK, head_local, head_size)
    third_slot = jnp.stack([padded[:, 5], padded[:, 0]], axis=1)
    far_keys = jnp.concatenate([padded[:, 0:2], padded[:, 4:6], third_slot], axis=2)
    first_index = device_index * half_blocks + jnp.arange(half_blocks, dtype=jnp.int32)
    valid = slot_masks(first_index, half_blocks * seq_count, 1, BLOCK)
    results.append(
        (
            1,
            level_attend(
                first_queries.reshape(half_blocks, BLOCK, head_local, head_size),
                far_keys[0],
                far_keys[1],
                valid,
                1,
                scale,
            ),
        )
    )
    queries_at = {}
    pieces = {}
    for level_index in range(2, top_level + 1):
        queries_at[level_index] = coarsen(query_rows, level_index, True)
        pieces[level_index] = jnp.stack(
            [coarsen(key_rows, level_index, True), coarsen(value_rows, level_index, False)]
        )
    shift_levels = list(range(2, top_level - 2))
    assembled = assemble_joint(pieces, shift_levels, device_index)
    for level_index in shift_levels:
        group = 1 << level_index - 2
        whole_block = assembled[level_index]
        before_two = shifted(whole_block, "seq", 2 * group)
        after_two = shifted(whole_block, "seq", -2 * group)
        block_index = device_index // group
        outgoing = jnp.where(block_index % 2 == 0, before_two, after_two)
        third_block = partner_2(outgoing, "seq", level_index - 2)
        level_keys = jnp.concatenate([before_two, after_two, third_block], axis=1)[:, None]
        valid = slot_masks(jnp.reshape(block_index, (1,)), seq_count // group, level_index, BLOCK)
        results.append(
            (
                level_index,
                level_attend(
                    queries_at[level_index][None],
                    level_keys[0],
                    level_keys[1],
                    valid,
                    level_index,
                    scale,
                ),
            )
        )
    coarse_list = [top_level - 2, top_level - 1, top_level]
    lines = lax.all_gather(
        jnp.concatenate([pieces[level_index].reshape(-1) for level_index in coarse_list]), "seq"
    )
    at = 0
    for level_index in coarse_list:
        group = 1 << level_index - 2
        block_total = seq_count // group
        rows = pieces[level_index].shape[1]
        size = pieces[level_index].size
        block_index = device_index // group
        targets = slot_targets(block_index, level_index)
        chosen = []
        for target in targets:
            part = lax.dynamic_slice_in_dim(
                lines, jnp.clip(target, 0, block_total - 1) * group, group, axis=0
            )
            part = part[:, at : at + size].reshape(group, 2, rows, head_local, head_size)
            chosen.append(jnp.moveaxis(part, 1, 0).reshape(2, group * rows, head_local, head_size))
        at += size
        level_keys = jnp.concatenate(chosen, axis=1)[:, None]
        valid = slot_masks(jnp.reshape(block_index, (1,)), block_total, level_index, BLOCK)
        results.append(
            (
                level_index,
                level_attend(
                    queries_at[level_index][None],
                    level_keys[0],
                    level_keys[1],
                    valid,
                    level_index,
                    scale,
                ),
            )
        )
    expanded = []
    for level_index, terms in results:
        factor = 1 << level_index
        expanded.append(
            (
                jnp.repeat(terms[0], factor, axis=0),
                jnp.repeat(terms[1], factor, axis=0),
                jnp.repeat(terms[2], factor, axis=0),
            )
        )
    overall = expanded[0][0]
    for entry in expanded[1:]:
        overall = jnp.maximum(overall, entry[0])
    weighted = jnp.zeros((token_count, head_local, head_size), jnp.float32)
    total_weight = jnp.zeros((token_count, head_local), jnp.float32)
    for part_peak, numerator, denominator in expanded:
        level_factor = jnp.exp(part_peak - overall)
        weighted = weighted + level_factor[:, :, None] * numerator
        total_weight = total_weight + level_factor * denominator
    attended = (weighted / total_weight[:, :, None]).astype(jnp.bfloat16)
    flattened = attended.reshape(token_count, head_local * head_size)
    weight_flat = out_weight.reshape(head_local * head_size, out_weight.shape[2])
    partial_value = jnp.dot(flattened, weight_flat, preferred_element_type=jnp.float32)
    return summed_on_arrival(partial_value.astype(jnp.bfloat16), "head", 1).astype(jnp.bfloat16)


def solution(mesh):
    return jax.shard_map(
        per_device,
        mesh=mesh,
        in_specs=(
            P("seq", "head", None),
            P("seq", "head", None),
            P("seq", "head", None),
            P("head", None, None),
        ),
        out_specs=P("seq", "head"),
        check_vma=False,
    )
```

```python
import jax
import jax.numpy as jnp
from jax import lax
from jax.sharding import PartitionSpec as P

BLOCK = 128


def partner_2(value, axis, distance):
    mask = 2**distance
    pairs = [(source, source ^ mask) for source in range(lax.axis_size(axis))]
    return lax.ppermute(value, axis, pairs)


def with_halo(value, sides, width):
    for axis, dim in sides:
        size, length = (lax.axis_size(axis), value.shape[dim])
        up = [(i, (i + 1) % size) for i in range(size - 1)]
        down = [(j, i) for i, j in up]
        last = lax.slice_in_dim(value, length - width, length, axis=dim)
        initial = lax.slice_in_dim(value, 0, width, axis=dim)
        before = lax.ppermute(last, axis, up)
        after = lax.ppermute(initial, axis, down)
        value = jnp.concatenate([before, value, after], axis=dim)
    return value


def shifted(value, axis, steps):
    count = lax.axis_size(axis)
    initial, last = (max(0, -steps), min(count, count - steps))
    return lax.ppermute(value, axis, [(source, source + steps) for source in range(initial, last)])


def joined_along(parts, dim):
    parts = jnp.moveaxis(parts, 0, dim)
    shape = parts.shape
    return parts.reshape(*shape[:dim], shape[dim] * shape[dim + 1], *shape[dim + 2 :])


def gather_packed(arrays, axis, dims):
    ravelled = jnp.concatenate([a.reshape(-1) for a in arrays])
    lines, at, done = (lax.all_gather(ravelled, axis), 0, [])
    for a, dim in zip(arrays, dims):
        parts = lines[:, at : at + a.size].reshape(-1, *a.shape)
        done.append(joined_along(parts, dim))
        at += a.size
    return tuple(done)


def cut_along(value, dim, length):
    shape = value.shape
    parts = value.reshape(*shape[:dim], length, shape[dim] // length, *shape[dim + 1 :])
    return jnp.moveaxis(parts, dim, 0)


def summed_on_arrival(value, axis, dim):
    length = lax.axis_size(axis)
    parts = lax.all_to_all(cut_along(value, dim, length), axis, 0, 0, tiled=True)
    return jnp.sum(parts.astype(jnp.float32), axis=0)


def coarsen(source, level_index, average):
    count = source.shape[0] >> level_index
    grouped = source.astype(jnp.float32).reshape((count, 1 << level_index) + source.shape[1:])
    summed = jnp.sum(grouped, axis=1)
    if average:
        summed = summed / float(1 << level_index)
    return summed.astype(jnp.bfloat16)


def slot_targets(block_index, level_index):
    if level_index == 0:
        return [block_index - 1, block_index, block_index + 1]
    return [
        block_index - 2,
        block_index + 2,
        jnp.where(block_index % 2 == 0, block_index + 3, block_index - 3),
    ]


def slot_masks(block_index, block_total, level_index, width):
    targets = slot_targets(block_index, level_index)
    return jnp.concatenate(
        [
            jnp.repeat(((target >= 0) & (target < block_total))[:, None], width, axis=1)
            for target in targets
        ],
        axis=1,
    )


def level_attend(query_blocks, key_blocks, value_blocks, valid, level_index, scale):
    scores = (
        jnp.einsum("nqhd,nkhd->nhqk", query_blocks, key_blocks, preferred_element_type=jnp.float32)
        * scale
    )
    scores = jnp.where(valid[:, None, None, :], scores, -jnp.inf)
    row_peak = jnp.max(scores, axis=3, keepdims=True)
    weights = jnp.exp(scores - row_peak)
    denominator = float(1 << level_index) * jnp.sum(weights, axis=3)
    numerator = jnp.einsum(
        "nhqk,nkhd->nqhd",
        weights.astype(jnp.bfloat16),
        value_blocks,
        preferred_element_type=jnp.float32,
    )
    block_count = query_blocks.shape[0]
    row_count = query_blocks.shape[1]
    peak_rows = jnp.transpose(row_peak[..., 0], (0, 2, 1)).reshape(block_count * row_count, -1)
    denominator_rows = jnp.transpose(denominator, (0, 2, 1)).reshape(block_count * row_count, -1)
    numerator_rows = numerator.reshape(
        block_count * row_count, numerator.shape[2], numerator.shape[3]
    )
    return (peak_rows, numerator_rows, denominator_rows)


def upper_half(device_index, bit):
    return device_index // (1 << bit) % 2 == 1


def assemble_joint(pieces, level_list, device_index):
    current = {}
    for level_index in level_list:
        current[level_index] = pieces[level_index]
    deepest = max([level_index - 2 for level_index in level_list] + [0])
    for bit in range(deepest):
        members = [level_index for level_index in level_list if level_index - 2 > bit]
        widths = [current[level_index].shape[1] for level_index in members]
        joined = jnp.concatenate([current[level_index] for level_index in members], axis=1)
        partner = partner_2(joined, "seq", bit)
        upper = upper_half(device_index, bit)
        offset = 0
        for level_index, width in zip(members, widths):
            theirs = partner[:, offset : offset + width]
            offset = offset + width
            mine = current[level_index]
            current[level_index] = jnp.concatenate([mine, theirs], axis=1)
    return current


def per_device(query_rows, key_rows, value_rows, out_weight):
    seq_count = lax.axis_size("seq")
    device_index = lax.axis_index("seq")
    token_count, head_local, head_size = query_rows.shape
    scale = float(head_size) ** (-0.5)
    top_level = seq_count.bit_length() - 1
    results = []
    local_blocks = token_count // BLOCK
    padded = with_halo(jnp.stack([key_rows, value_rows]), (("seq", 1),), BLOCK)
    padded = padded.reshape(2, local_blocks + 2, BLOCK, head_local, head_size)
    near_keys = jnp.concatenate(
        [
            padded[:, 0:local_blocks],
            padded[:, 1 : local_blocks + 1],
            padded[:, 2 : local_blocks + 2],
        ],
        axis=2,
    )
    fine_index = device_index * local_blocks + jnp.arange(local_blocks, dtype=jnp.int32)
    valid = slot_masks(fine_index, local_blocks * seq_count, 0, BLOCK)
    results.append(
        (
            0,
            level_attend(
                query_rows.reshape(local_blocks, BLOCK, head_local, head_size),
                near_keys[0],
                near_keys[1],
                valid,
                0,
                scale,
            ),
        )
    )
    half_blocks = local_blocks // 2
    first_queries = coarsen(query_rows, 1, True)
    first_pair = jnp.stack([coarsen(key_rows, 1, True), coarsen(value_rows, 1, False)])
    padded = with_halo(first_pair, (("seq", 1),), first_pair.shape[1])
    padded = padded.reshape(2, 3 * half_blocks, BLOCK, head_local, head_size)
    third_slot = jnp.stack([padded[:, 5], padded[:, 0]], axis=1)
    far_keys = jnp.concatenate([padded[:, 0:2], padded[:, 4:6], third_slot], axis=2)
    first_index = device_index * half_blocks + jnp.arange(half_blocks, dtype=jnp.int32)
    valid = slot_masks(first_index, half_blocks * seq_count, 1, BLOCK)
    results.append(
        (
            1,
            level_attend(
                first_queries.reshape(half_blocks, BLOCK, head_local, head_size),
                far_keys[0],
                far_keys[1],
                valid,
                1,
                scale,
            ),
        )
    )
    queries_at = {}
    pieces = {}
    for level_index in range(2, top_level + 1):
        queries_at[level_index] = coarsen(query_rows, level_index, True)
        pieces[level_index] = jnp.stack(
            [coarsen(key_rows, level_index, True), coarsen(value_rows, level_index, False)]
        )
    shift_levels = list(range(2, top_level - 2))
    assembled = assemble_joint(pieces, shift_levels, device_index)
    for level_index in shift_levels:
        group = 1 << level_index - 2
        whole_block = assembled[level_index]
        before_two = shifted(whole_block, "seq", 2 * group)
        after_two = shifted(whole_block, "seq", -2 * group)
        block_index = device_index // group
        outgoing = jnp.where(block_index % 2 == 0, before_two, after_two)
        third_block = partner_2(outgoing, "seq", level_index - 2)
        level_keys = jnp.concatenate([before_two, after_two, third_block], axis=1)[:, None]
        valid = slot_masks(jnp.reshape(block_index, (1,)), seq_count // group, level_index, BLOCK)
        results.append(
            (
                level_index,
                level_attend(
                    queries_at[level_index][None],
                    level_keys[0],
                    level_keys[1],
                    valid,
                    level_index,
                    scale,
                ),
            )
        )
    coarse_list = [top_level - 2, top_level - 1, top_level]
    lines = lax.all_gather(
        jnp.concatenate(
            [pieces[level_index].reshape(-1, head_size) for level_index in coarse_list]
        ),
        "seq",
    )
    at = 0
    for level_index in coarse_list:
        group = 1 << level_index - 2
        block_total = seq_count // group
        rows = pieces[level_index].shape[1]
        size = pieces[level_index].size // head_size
        block_index = device_index // group
        targets = slot_targets(block_index, level_index)
        chosen = []
        for target in targets:
            part = lax.dynamic_slice_in_dim(
                lines, jnp.clip(target, 0, block_total - 1) * group, group, axis=0
            )
            part = part[:, at : at + size].reshape(group, 2, rows, head_local, head_size)
            chosen.append(jnp.moveaxis(part, 1, 0).reshape(2, group * rows, head_local, head_size))
        at += size
        level_keys = jnp.concatenate(chosen, axis=1)[:, None]
        valid = slot_masks(jnp.reshape(block_index, (1,)), block_total, level_index, BLOCK)
        results.append(
            (
                level_index,
                level_attend(
                    queries_at[level_index][None],
                    level_keys[0],
                    level_keys[1],
                    valid,
                    level_index,
                    scale,
                ),
            )
        )
    expanded = []
    for level_index, terms in results:
        factor = 1 << level_index
        expanded.append(
            (
                jnp.repeat(terms[0], factor, axis=0),
                jnp.repeat(terms[1], factor, axis=0),
                jnp.repeat(terms[2], factor, axis=0),
            )
        )
    overall = expanded[0][0]
    for entry in expanded[1:]:
        overall = jnp.maximum(overall, entry[0])
    weighted = jnp.zeros((token_count, head_local, head_size), jnp.float32)
    total_weight = jnp.zeros((token_count, head_local), jnp.float32)
    for part_peak, numerator, denominator in expanded:
        level_factor = jnp.exp(part_peak - overall)
        weighted = weighted + level_factor[:, :, None] * numerator
        total_weight = total_weight + level_factor * denominator
    attended = (weighted / total_weight[:, :, None]).astype(jnp.bfloat16)
    flattened = attended.reshape(token_count, head_local * head_size)
    weight_flat = out_weight.reshape(head_local * head_size, out_weight.shape[2])
    partial_value = jnp.dot(flattened, weight_flat, preferred_element_type=jnp.float32)
    return summed_on_arrival(partial_value.astype(jnp.bfloat16), "head", 1).astype(jnp.bfloat16)


def solution(mesh):
    return jax.shard_map(
        per_device,
        mesh=mesh,
        in_specs=(
            P("seq", "head", None),
            P("seq", "head", None),
            P("seq", "head", None),
            P("head", None, None),
        ),
        out_specs=P("seq", "head"),
        check_vma=False,
    )
```

```python
import jax
import jax.numpy as jnp
from jax import lax
from jax.sharding import PartitionSpec as P

BLOCK = 128


def partner_2(value, axis, distance):
    mask = 2**distance
    pairs = [(source, source ^ mask) for source in range(lax.axis_size(axis))]
    return lax.ppermute(value, axis, pairs)


def with_halo(value, sides, width):
    for axis, dim in sides:
        size, length = (lax.axis_size(axis), value.shape[dim])
        up = [(i, (i + 1) % size) for i in range(size - 1)]
        down = [(j, i) for i, j in up]
        last = lax.slice_in_dim(value, length - width, length, axis=dim)
        initial = lax.slice_in_dim(value, 0, width, axis=dim)
        before = lax.ppermute(last, axis, up)
        after = lax.ppermute(initial, axis, down)
        value = jnp.concatenate([before, value, after], axis=dim)
    return value


def shifted(value, axis, steps):
    count = lax.axis_size(axis)
    initial, last = (max(0, -steps), min(count, count - steps))
    return lax.ppermute(value, axis, [(source, source + steps) for source in range(initial, last)])


def joined_along(parts, dim):
    parts = jnp.moveaxis(parts, 0, dim)
    shape = parts.shape
    return parts.reshape(*shape[:dim], shape[dim] * shape[dim + 1], *shape[dim + 2 :])


def gather_packed(arrays, axis, dims):
    ravelled = jnp.concatenate([a.reshape(-1) for a in arrays])
    lines, at, done = (lax.all_gather(ravelled, axis), 0, [])
    for a, dim in zip(arrays, dims):
        parts = lines[:, at : at + a.size].reshape(-1, *a.shape)
        done.append(joined_along(parts, dim))
        at += a.size
    return tuple(done)


def cut_along(value, dim, length):
    shape = value.shape
    parts = value.reshape(*shape[:dim], length, shape[dim] // length, *shape[dim + 1 :])
    return jnp.moveaxis(parts, dim, 0)


def summed_on_arrival(value, axis, dim):
    length = lax.axis_size(axis)
    parts = lax.all_to_all(cut_along(value, dim, length), axis, 0, 0, tiled=True)
    return jnp.sum(parts.astype(jnp.float32), axis=0)


def coarsen(source, level_index, average):
    count = source.shape[0] >> level_index
    grouped = source.astype(jnp.float32).reshape((count, 1 << level_index) + source.shape[1:])
    summed = jnp.sum(grouped, axis=1)
    if average:
        summed = summed / float(1 << level_index)
    return summed.astype(jnp.bfloat16)


def slot_targets(block_index, level_index):
    if level_index == 0:
        return [block_index - 1, block_index, block_index + 1]
    return [
        block_index - 2,
        block_index + 2,
        jnp.where(block_index % 2 == 0, block_index + 3, block_index - 3),
    ]


def slot_masks(block_index, block_total, level_index, width):
    targets = slot_targets(block_index, level_index)
    return jnp.concatenate(
        [
            jnp.repeat(((target >= 0) & (target < block_total))[:, None], width, axis=1)
            for target in targets
        ],
        axis=1,
    )


def level_attend(query_blocks, key_blocks, value_blocks, valid, level_index, scale):
    scores = (
        jnp.einsum("nqhd,nkhd->nhqk", query_blocks, key_blocks, preferred_element_type=jnp.float32)
        * scale
    )
    scores = jnp.where(valid[:, None, None, :], scores, -jnp.inf)
    row_peak = jnp.max(scores, axis=3, keepdims=True)
    weights = jnp.exp(scores - row_peak)
    denominator = float(1 << level_index) * jnp.sum(weights, axis=3)
    numerator = jnp.einsum(
        "nhqk,nkhd->nqhd",
        weights.astype(jnp.bfloat16),
        value_blocks,
        preferred_element_type=jnp.float32,
    )
    block_count = query_blocks.shape[0]
    row_count = query_blocks.shape[1]
    peak_rows = jnp.transpose(row_peak[..., 0], (0, 2, 1)).reshape(block_count * row_count, -1)
    denominator_rows = jnp.transpose(denominator, (0, 2, 1)).reshape(block_count * row_count, -1)
    numerator_rows = numerator.reshape(
        block_count * row_count, numerator.shape[2], numerator.shape[3]
    )
    return (peak_rows, numerator_rows, denominator_rows)


def upper_half(device_index, bit):
    return device_index // (1 << bit) % 2 == 1


def assemble_joint(pieces, level_list, device_index):
    current = {}
    for level_index in level_list:
        current[level_index] = pieces[level_index]
    deepest = max([level_index - 2 for level_index in level_list] + [0])
    for bit in range(deepest):
        members = [level_index for level_index in level_list if level_index - 2 > bit]
        widths = [current[level_index].shape[1] for level_index in members]
        joined = jnp.concatenate([current[level_index] for level_index in members], axis=1)
        partner = partner_2(joined, "seq", bit)
        upper = upper_half(device_index, bit)
        offset = 0
        for level_index, width in zip(members, widths):
            theirs = partner[:, offset : offset + width]
            offset = offset + width
            mine = current[level_index]
            current[level_index] = jnp.concatenate([mine, theirs], axis=1)
    return current


def per_device(query_rows, key_rows, value_rows, out_weight):
    seq_count = lax.axis_size("seq")
    device_index = lax.axis_index("seq")
    token_count, head_local, head_size = query_rows.shape
    scale = float(head_size) ** (-0.5)
    top_level = seq_count.bit_length() - 1
    results = []
    local_blocks = token_count // BLOCK
    padded = with_halo(jnp.stack([key_rows, value_rows]), (("seq", 1),), BLOCK)
    padded = padded.reshape(2, local_blocks + 2, BLOCK, head_local, head_size)
    near_keys = jnp.concatenate(
        [
            padded[:, 0:local_blocks],
            padded[:, 1 : local_blocks + 1],
            padded[:, 2 : local_blocks + 2],
        ],
        axis=2,
    )
    fine_index = device_index * local_blocks + jnp.arange(local_blocks, dtype=jnp.int32)
    valid = slot_masks(fine_index, local_blocks * seq_count, 0, BLOCK)
    results.append(
        (
            0,
            level_attend(
                query_rows.reshape(local_blocks, BLOCK, head_local, head_size),
                near_keys[0],
                near_keys[1],
                valid,
                0,
                scale,
            ),
        )
    )
    half_blocks = local_blocks // 2
    first_queries = coarsen(query_rows, 1, True)
    first_pair = jnp.stack([coarsen(key_rows, 1, True), coarsen(value_rows, 1, False)])
    padded = with_halo(first_pair, (("seq", 1),), first_pair.shape[1])
    padded = padded.reshape(2, 3 * half_blocks, BLOCK, head_local, head_size)
    third_slot = jnp.stack([padded[:, 5], padded[:, 0]], axis=1)
    far_keys = jnp.concatenate([padded[:, 0:2], padded[:, 4:6], third_slot], axis=2)
    first_index = device_index * half_blocks + jnp.arange(half_blocks, dtype=jnp.int32)
    valid = slot_masks(first_index, half_blocks * seq_count, 1, BLOCK)
    results.append(
        (
            1,
            level_attend(
                first_queries.reshape(half_blocks, BLOCK, head_local, head_size),
                far_keys[0],
                far_keys[1],
                valid,
                1,
                scale,
            ),
        )
    )
    queries_at = {}
    pieces = {}
    for level_index in range(2, top_level + 1):
        queries_at[level_index] = coarsen(query_rows, level_index, True)
        pieces[level_index] = jnp.stack(
            [coarsen(key_rows, level_index, True), coarsen(value_rows, level_index, False)]
        )
    shift_levels = list(range(2, top_level - 3))
    assembled = assemble_joint(pieces, shift_levels, device_index)
    for level_index in shift_levels:
        group = 1 << level_index - 2
        whole_block = assembled[level_index]
        before_two = shifted(whole_block, "seq", 2 * group)
        after_two = shifted(whole_block, "seq", -2 * group)
        block_index = device_index // group
        outgoing = jnp.where(block_index % 2 == 0, before_two, after_two)
        third_block = partner_2(outgoing, "seq", level_index - 2)
        level_keys = jnp.concatenate([before_two, after_two, third_block], axis=1)[:, None]
        valid = slot_masks(jnp.reshape(block_index, (1,)), seq_count // group, level_index, BLOCK)
        results.append(
            (
                level_index,
                level_attend(
                    queries_at[level_index][None],
                    level_keys[0],
                    level_keys[1],
                    valid,
                    level_index,
                    scale,
                ),
            )
        )
    coarse_list = [top_level - 3, top_level - 2, top_level - 1, top_level]
    lines = lax.all_gather(
        jnp.concatenate(
            [pieces[level_index].reshape(-1, head_size) for level_index in coarse_list]
        ),
        "seq",
    )
    at = 0
    for level_index in coarse_list:
        group = 1 << level_index - 2
        block_total = seq_count // group
        rows = pieces[level_index].shape[1]
        size = pieces[level_index].size // head_size
        block_index = device_index // group
        targets = slot_targets(block_index, level_index)
        chosen = []
        for target in targets:
            part = lax.dynamic_slice_in_dim(
                lines, jnp.clip(target, 0, block_total - 1) * group, group, axis=0
            )
            part = part[:, at : at + size].reshape(group, 2, rows, head_local, head_size)
            chosen.append(jnp.moveaxis(part, 1, 0).reshape(2, group * rows, head_local, head_size))
        at += size
        level_keys = jnp.concatenate(chosen, axis=1)[:, None]
        valid = slot_masks(jnp.reshape(block_index, (1,)), block_total, level_index, BLOCK)
        results.append(
            (
                level_index,
                level_attend(
                    queries_at[level_index][None],
                    level_keys[0],
                    level_keys[1],
                    valid,
                    level_index,
                    scale,
                ),
            )
        )
    expanded = []
    for level_index, terms in results:
        factor = 1 << level_index
        expanded.append(
            (
                jnp.repeat(terms[0], factor, axis=0),
                jnp.repeat(terms[1], factor, axis=0),
                jnp.repeat(terms[2], factor, axis=0),
            )
        )
    overall = expanded[0][0]
    for entry in expanded[1:]:
        overall = jnp.maximum(overall, entry[0])
    weighted = jnp.zeros((token_count, head_local, head_size), jnp.float32)
    total_weight = jnp.zeros((token_count, head_local), jnp.float32)
    for part_peak, numerator, denominator in expanded:
        level_factor = jnp.exp(part_peak - overall)
        weighted = weighted + level_factor[:, :, None] * numerator
        total_weight = total_weight + level_factor * denominator
    attended = (weighted / total_weight[:, :, None]).astype(jnp.bfloat16)
    flattened = attended.reshape(token_count, head_local * head_size)
    weight_flat = out_weight.reshape(head_local * head_size, out_weight.shape[2])
    partial_value = jnp.dot(flattened, weight_flat, preferred_element_type=jnp.float32)
    return summed_on_arrival(partial_value.astype(jnp.bfloat16), "head", 1).astype(jnp.bfloat16)


def solution(mesh):
    return jax.shard_map(
        per_device,
        mesh=mesh,
        in_specs=(
            P("seq", "head", None),
            P("seq", "head", None),
            P("seq", "head", None),
            P("head", None, None),
        ),
        out_specs=P("seq", "head"),
        check_vma=False,
    )
```
